128 devices in a mesh: dp: 4 (over x), expert: 32 (over y, z, core).
Axes of the slice: x: 4, y: 4, z: 4, core: 2. Of those that a mesh axis runs over, the one named last changes fastest.
Arguments:
- tokens: bfloat16 [16384, 4096], P(('dp', 'expert')), may hold values from -6 to 6
- cotangent: bfloat16 [16384, 4096], P(('dp', 'expert')), may hold values from -6 to 6
- routes: int32 [16384], P(('dp', 'expert')), may hold values from 0 to 31, as said below
- combine: float32 [16384], P(('dp', 'expert')), may hold values from 0.05 to 1
- expert_weights: bfloat16 [32, 3, 1536, 4096], P('expert', None, 'dp'), may hold values from -0.09375 to 0.09375
Outputs:
- combined: bfloat16 [16384, 4096], P(('dp', 'expert'))
- token_grad: bfloat16 [16384, 4096], P(('dp', 'expert'))
- combine_grad: float32 [16384], P(('dp', 'expert'))
The draws below stay inside these ranges and needn't reach their ends.
Inputs may be any that keep to these rules, and one draw needn't show every extreme that they name: `routes`: among the 128 rows of every device, two experts, the same two on every device, are each named by exactly 8 rows, and every other expert by 3 or 4 rows.
All inputs are finite; a program needn't handle non-finite values.
Results may differ from the reference program's by a relative error of at most 0.015.
Values may be sent and summed in bfloat16 or wider, within the bound.
No kernel may reach another device: no remote copies, remote signals or barrier semaphores. Data moves between devices by JAX's collectives and lax.ppermute only.
A program may use at most 192 MiB of HBM per device.

```python
import math
import jax
import jax.numpy as jnp
from jax import lax

D = 4096
FF = 1536
TOK_DEV = 128
EXPERTS = 32
TOKENS = 16384
CAP = 8
N_DP = 4
N_EXPERT = 32


def draw_routes(key, part):
    block_total = TOKENS // TOK_DEV
    order = jax.random.permutation(jax.random.fold_in(key, 7), EXPERTS).astype(jnp.int32)
    position = jnp.arange(TOK_DEV, dtype=jnp.int32)

    def one_block(block_key):
        shift_key, order_key = jax.random.split(block_key)
        offset = jax.random.randint(shift_key, (), 0, EXPERTS - 2).astype(jnp.int32)
        cold_ids = order[2 + (position - 2 * CAP + offset) % (EXPERTS - 2)]
        labels = jnp.where(position < CAP, order[0], jnp.where(position < 2 * CAP, order[1], cold_ids))
        return labels[jax.random.permutation(order_key, TOK_DEV)]
    block_keys = jax.random.split(jax.random.fold_in(key, 11), block_total)
    return jax.vmap(one_block)(block_keys).reshape(TOKENS).astype(jnp.int32)


def levels(own_key, extent, shards, least, high):
    gain, own = 1.0, jax.random.fold_in(own_key, 6)
    for dim, blocks in shards:
        draws = jnp.exp(jax.random.uniform(jax.random.fold_in(own, dim), (blocks,), jnp.float32, least / len(shards), high / len(shards)))
        gain = gain * jnp.repeat(draws, extent[dim] // blocks).reshape([-1 if axis == dim else 1 for axis in range(len(extent))])
    return gain


def scatter_about(rng, dims, spread, most, cuts=(), held_as=jnp.bfloat16):
    result = spread * jax.random.normal(rng, dims, jnp.float32)
    if cuts:
        result = result * levels(rng, dims, cuts, -0.22, 0.18)
    return jnp.clip(result, -most, most).astype(held_as)


def setup_inputs(seed: int = 0) -> dict:
    arg_keys = jax.random.split(jax.random.key(seed), 6)
    tokens = scatter_about(arg_keys[0], (TOKENS, D), 1.0, 6.0, ((0, 128),))
    cotangent = scatter_about(arg_keys[1], (TOKENS, D), 1.0, 6.0, ((0, 128),))
    routes = draw_routes(jax.random.fold_in(arg_keys[5], 71), 0)
    combine = jnp.clip(jnp.exp(math.log(1.0) - 2.9957323 * jax.random.uniform(arg_keys[3], (TOKENS,), jnp.float32) ** levels(arg_keys[3], (TOKENS,), ((0, 128),), -0.2, 0.2)), 0.05, 1.0)
    expert_weights = scatter_about(arg_keys[4], (EXPERTS, 3, FF, D), D ** -0.5, 0.09375, ((0, 32), (2, 4)))
    return dict(tokens=tokens, cotangent=cotangent, routes=routes, combine=combine, expert_weights=expert_weights)


def settle(parts):
    rounded = lax.optimization_barrier(parts.astype(jnp.bfloat16))
    return jnp.sum(rounded.astype(jnp.float32), 0).astype(jnp.bfloat16)


def expert_pass(expert_id, tokens, cotangent, routes, combine, expert_weights):
    row_total = CAP * N_DP * N_EXPERT
    group_width = FF // N_DP
    chosen = jnp.argsort((routes != expert_id).astype(jnp.int32), stable=True)[:row_total].astype(jnp.int32)
    is_valid = routes[chosen] == expert_id
    matrices = lax.dynamic_index_in_dim(expert_weights, expert_id, 0, keepdims=False).astype(jnp.float32)
    picked = tokens[chosen].astype(jnp.float32)
    gate_act = jnp.dot(picked, matrices[0].T)
    up_act = jnp.dot(picked, matrices[1].T)
    squashed = jax.nn.sigmoid(gate_act)
    hidden = (gate_act * squashed * up_act).astype(jnp.bfloat16)
    hidden_groups = hidden.astype(jnp.float32).reshape(row_total, N_DP, group_width)
    down_parts = jnp.einsum("rqf,qfd->qrd", hidden_groups, matrices[2].reshape(N_DP, group_width, D))
    expert_out = settle(down_parts)
    out_grad = (combine[chosen][:, None] * cotangent[chosen].astype(jnp.float32)).astype(jnp.bfloat16)
    hidden_grad = jnp.dot(out_grad.astype(jnp.float32), matrices[2].T)
    gate_grad = (hidden_grad * up_act * squashed * (1.0 + gate_act * (1.0 - squashed))).astype(jnp.bfloat16)
    up_grad = (hidden_grad * gate_act * squashed).astype(jnp.bfloat16)
    gate_groups = gate_grad.astype(jnp.float32).reshape(row_total, N_DP, group_width)
    up_groups = up_grad.astype(jnp.float32).reshape(row_total, N_DP, group_width)
    input_parts = jnp.einsum("rqf,qfd->qrd", gate_groups, matrices[0].reshape(N_DP, group_width, D))
    input_parts = input_parts + jnp.einsum("rqf,qfd->qrd", up_groups, matrices[1].reshape(N_DP, group_width, D))
    input_grad = settle(input_parts)
    keep = is_valid[:, None]
    return chosen, jnp.where(keep, expert_out.astype(jnp.float32), 0.0), jnp.where(keep, input_grad.astype(jnp.float32), 0.0)


def reference(tokens, cotangent, routes, combine, expert_weights):
    def one_expert(totals, expert_id):
        chosen, expert_out, input_grad = expert_pass(expert_id, tokens, cotangent, routes, combine, expert_weights)
        out_total = totals[0].at[chosen].add(expert_out)
        grad_total = totals[1].at[chosen].add(input_grad)
        return (out_total, grad_total), None

    start = (jnp.zeros((TOKENS, D), jnp.float32), jnp.zeros((TOKENS, D), jnp.float32))
    totals, _ = lax.scan(one_expert, start, jnp.arange(EXPERTS, dtype=jnp.int32))
    expert_out = totals[0]
    combined = (combine[:, None] * expert_out).astype(jnp.bfloat16)
    combine_grad = jnp.sum(expert_out * cotangent.astype(jnp.float32), 1)
    token_grad = totals[1].astype(jnp.bfloat16)
    return combined, token_grad, combine_grad
```

```python
import jax
import jax.numpy as jnp
from jax import lax
from jax.sharding import PartitionSpec as P


def placement(member, slot_count):
    within = jnp.sum((jnp.cumsum(member, 0) - 1) * member, 1)
    owner_group = jnp.sum(member * lax.iota(jnp.int32, member.shape[1])[None, :], 1)
    is_used = jnp.sum(member, 1) > 0
    target = owner_group * slot_count + within
    buffer_cells = lax.iota(jnp.int32, member.shape[1] * slot_count)
    return ((buffer_cells[:, None] == target[None, :]) & is_used[None, :]).astype(jnp.bfloat16)


def spread(layout, row_block):
    return jnp.dot(layout, row_block, preferred_element_type=jnp.float32).astype(jnp.bfloat16)


def collect(layout, buffer_rows):
    return lax.dot_general(
        layout, buffer_rows, (((0,), (0,)), ((), ())), preferred_element_type=jnp.float32
    )


def group_rows(values):
    return lax.all_gather(values, "dp", axis=0, tiled=True)


def group_sum(values):
    return lax.psum_scatter(
        values.astype(jnp.bfloat16), "dp", scatter_dimension=0, tiled=True
    )


def exchange(rows, experts, model_width):
    return lax.all_to_all(
        rows.reshape(experts, -1, model_width), "expert", split_axis=0, concat_axis=0, tiled=True
    ).reshape(-1, model_width)


def forward_rows(row_block, matrices):
    gate_up = jnp.einsum("rd,kfd->krf", row_block, matrices[:2], preferred_element_type=jnp.float32)
    gate_act = gate_up[0]
    up_act = gate_up[1]
    hidden = (gate_act * jax.nn.sigmoid(gate_act) * up_act).astype(jnp.bfloat16)
    partial_out = jnp.dot(hidden, matrices[2], preferred_element_type=jnp.float32)
    return (gate_act, up_act, partial_out)


def backward_rows(row_block, gate_act, up_act, matrices):
    hidden_grad = lax.dot_general(
        row_block, matrices[2], (((1,), (1,)), ((), ())), preferred_element_type=jnp.float32
    )
    squashed = jax.nn.sigmoid(gate_act)
    gate_grad = (hidden_grad * up_act * squashed * (1.0 + gate_act * (1.0 - squashed))).astype(
        jnp.bfloat16
    )
    up_grad = (hidden_grad * gate_act * squashed).astype(jnp.bfloat16)
    both_grads = jnp.stack([gate_grad, up_grad])
    return jnp.einsum("krf,kfd->rd", both_grads, matrices[:2], preferred_element_type=jnp.float32)


def shards(tokens, cotangent, routes, combine, expert_weights):
    weights = expert_weights[0]
    tok_dev = tokens.shape[0]
    model_width = tokens.shape[1]
    experts = lax.axis_size("expert")
    capacity = 2 * tok_dev // experts
    chunks = 2
    chunk_slots = capacity // chunks
    labels = lax.iota(jnp.int32, experts)
    member = (routes[:, None] == labels[None, :]).astype(jnp.int32)
    layout = placement(member, capacity).reshape(experts, capacity, tok_dev)
    cotangent_wide = cotangent.astype(jnp.float32)
    out_grad = (combine[:, None] * cotangent_wide).astype(jnp.bfloat16)

    layouts = [
        layout[:, c * chunk_slots:(c + 1) * chunk_slots].reshape(-1, tok_dev) for c in range(chunks)
    ]
    tok_in = [group_rows(exchange(spread(lay, tokens), experts, model_width)) for lay in layouts]
    cot_in = [group_rows(exchange(spread(lay, out_grad), experts, model_width)) for lay in layouts]
    expert_out = None
    input_grad = None
    for c in range(chunks):
        gate_act, up_act, part = forward_rows(tok_in[c], weights)
        out_back = exchange(group_sum(part), experts, model_width)
        piece = collect(layouts[c], out_back)
        expert_out = piece if expert_out is None else expert_out + piece
        grad_part = backward_rows(cot_in[c], gate_act, up_act, weights)
        grad_back = exchange(group_sum(grad_part), experts, model_width)
        piece = collect(layouts[c], grad_back)
        input_grad = piece if input_grad is None else input_grad + piece
    combined = (combine[:, None] * expert_out).astype(jnp.bfloat16)
    combine_grad = jnp.sum(expert_out * cotangent_wide, 1)
    token_grad = input_grad.astype(jnp.bfloat16)
    return (combined, token_grad, combine_grad)


def solution(mesh):
    return jax.shard_map(
        shards,
        mesh=mesh,
        in_specs=(
            P(("dp", "expert"), None),
            P(("dp", "expert"), None),
            P(("dp", "expert")),
            P(("dp", "expert")),
            P("expert", None, "dp", None),
        ),
        out_specs=(P(("dp", "expert"), None), P(("dp", "expert"), None), P(("dp", "expert"))),
        check_vma=False,
    )
```

```python
import jax
import jax.numpy as jnp
from jax import lax
from jax.sharding import PartitionSpec as P


def placement(member, slot_count):
    within = jnp.sum((jnp.cumsum(member, 0) - 1) * member, 1)
    owner_group = jnp.sum(member * lax.iota(jnp.int32, member.shape[1])[None, :], 1)
    is_used = jnp.sum(member, 1) > 0
    target = owner_group * slot_count + within
    buffer_cells = lax.iota(jnp.int32, member.shape[1] * slot_count)
    return ((buffer_cells[:, None] == target[None, :]) & is_used[None, :]).astype(jnp.bfloat16)


def spread(layout, row_block):
    return jnp.dot(layout, row_block, preferred_element_type=jnp.float32).astype(jnp.bfloat16)


def collect(layout, buffer_rows):
    return lax.dot_general(
        layout, buffer_rows, (((0,), (0,)), ((), ())), preferred_element_type=jnp.float32
    )


def group_rows(values):
    return lax.all_gather(values, "dp", axis=0, tiled=True)


def group_sum(values):
    return lax.psum_scatter(
        values.astype(jnp.bfloat16), "dp", scatter_dimension=0, tiled=True
    ).astype(jnp.float32)


def send_rows(cold_buf, experts, slot_count, model_width):
    arrived = lax.all_to_all(
        cold_buf.reshape(experts, slot_count, model_width),
        "expert",
        split_axis=0,
        concat_axis=0,
        tiled=True,
    ).reshape(-1, model_width)
    cold_in = group_rows(arrived)
    hot_in = None
    return (cold_in, hot_in)


def return_rows(cold_part, experts, slot_count, model_width):
    cold_total = group_sum(cold_part)
    hot_out = None
    summed = cold_total.astype(jnp.bfloat16).reshape(experts, slot_count, model_width)
    cold_out = lax.all_to_all(summed, "expert", split_axis=0, concat_axis=0, tiled=True).reshape(
        -1, model_width
    )
    return (cold_out, hot_out)


def forward_rows(row_block, matrices):
    gate_up = jnp.einsum("rd,kfd->krf", row_block, matrices[:2], preferred_element_type=jnp.float32)
    gate_act = gate_up[0]
    up_act = gate_up[1]
    hidden = (gate_act * jax.nn.sigmoid(gate_act) * up_act).astype(jnp.bfloat16)
    partial_out = jnp.dot(hidden, matrices[2], preferred_element_type=jnp.float32)
    return (gate_act, up_act, partial_out)


def backward_rows(row_block, gate_act, up_act, matrices):
    hidden_grad = lax.dot_general(
        row_block, matrices[2], (((1,), (1,)), ((), ())), preferred_element_type=jnp.float32
    )
    squashed = jax.nn.sigmoid(gate_act)
    gate_grad = (hidden_grad * up_act * squashed * (1.0 + gate_act * (1.0 - squashed))).astype(
        jnp.bfloat16
    )
    up_grad = (hidden_grad * gate_act * squashed).astype(jnp.bfloat16)
    both_grads = jnp.stack([gate_grad, up_grad])
    return jnp.einsum("krf,kfd->rd", both_grads, matrices[:2], preferred_element_type=jnp.float32)


def shards(tokens, cotangent, routes, combine, expert_weights):
    weights = expert_weights[0]
    tok_dev = tokens.shape[0]
    model_width = tokens.shape[1]
    experts = lax.axis_size("expert")
    capacity = 2 * tok_dev // experts
    labels = lax.iota(jnp.int32, experts)
    member = (routes[:, None] == labels[None, :]).astype(jnp.int32)
    cold_layout = placement(member, capacity)
    cold_buf = spread(cold_layout, tokens)
    cold_in, hot_in = send_rows(cold_buf, experts, capacity, model_width)
    gate_act, up_act, cold_part = forward_rows(cold_in, weights)
    cotangent_wide = cotangent.astype(jnp.float32)
    out_grad = (combine[:, None] * cotangent_wide).astype(jnp.bfloat16)
    cold_grad_buf = spread(cold_layout, out_grad)
    cold_grad_in, hot_grad_in = send_rows(cold_grad_buf, experts, capacity, model_width)
    cold_part = cold_part.astype(jnp.bfloat16)
    cold_part, cold_grad_in = lax.optimization_barrier((cold_part, cold_grad_in))
    cold_out, hot_out = return_rows(cold_part, experts, capacity, model_width)
    expert_out = collect(cold_layout, cold_out)
    combined = (combine[:, None] * expert_out).astype(jnp.bfloat16)
    combine_grad = jnp.sum(expert_out * cotangent_wide, 1)
    cold_grad_part = backward_rows(cold_grad_in, gate_act, up_act, weights)
    cold_grad_out, hot_grad_out = return_rows(cold_grad_part, experts, capacity, model_width)
    input_grad = collect(cold_layout, cold_grad_out)
    token_grad = input_grad.astype(jnp.bfloat16)
    return (combined, token_grad, combine_grad)


def solution(mesh):
    return jax.shard_map(
        shards,
        mesh=mesh,
        in_specs=(
            P(("dp", "expert"), None),
            P(("dp", "expert"), None),
            P(("dp", "expert")),
            P(("dp", "expert")),
            P("expert", None, "dp", None),
        ),
        out_specs=(P(("dp", "expert"), None), P(("dp", "expert"), None), P(("dp", "expert"))),
        check_vma=False,
    )
```

```python
import jax
import jax.numpy as jnp
from jax import lax
from jax.sharding import PartitionSpec as P


def placement(member, slot_count):
    within = jnp.sum((jnp.cumsum(member, 0) - 1) * member, 1)
    owner_group = jnp.sum(member * lax.iota(jnp.int32, member.shape[1])[None, :], 1)
    is_used = jnp.sum(member, 1) > 0
    target = owner_group * slot_count + within
    buffer_cells = lax.iota(jnp.int32, member.shape[1] * slot_count)
    return ((buffer_cells[:, None] == target[None, :]) & is_used[None, :]).astype(jnp.bfloat16)


def spread(layout, row_block):
    return jnp.dot(layout, row_block, preferred_element_type=jnp.float32).astype(jnp.bfloat16)


def collect(layout, buffer_rows):
    return lax.dot_general(
        layout, buffer_rows, (((0,), (0,)), ((), ())), preferred_element_type=jnp.float32
    )


def shifted(values, step):
    n = lax.axis_size("dp")
    return lax.ppermute(values, "dp", perm=[(i, (i + step) % n) for i in range(n)])


def group_rows(values):
    half = values.shape[0] // 2
    from_left = shifted(values, 1)
    from_right = shifted(values, -1)
    far_head = shifted(from_left[:half], 1)
    far_tail = shifted(from_right[half:], -1)
    return jnp.concatenate([values, from_left, from_right, far_head, far_tail], 0)


def group_sum(values):
    own, to_left, to_right, far = jnp.split(values, 4, 0)
    half = far.shape[0] // 2
    far_head = shifted(far[:half].astype(jnp.bfloat16), -1).astype(jnp.float32)
    far_tail = shifted(far[half:].astype(jnp.bfloat16), 1).astype(jnp.float32)
    to_left = to_left.astype(jnp.bfloat16).astype(jnp.float32)
    to_right = to_right.astype(jnp.bfloat16).astype(jnp.float32)
    to_left = jnp.concatenate([to_left[:half] + far_head, to_left[half:]], 0)
    to_right = jnp.concatenate([to_right[:half], to_right[half:] + far_tail], 0)
    back_right = shifted(to_left.astype(jnp.bfloat16), -1).astype(jnp.float32)
    back_left = shifted(to_right.astype(jnp.bfloat16), 1).astype(jnp.float32)
    return own.astype(jnp.bfloat16).astype(jnp.float32) + back_right + back_left


def send_rows(cold_buf, experts, slot_count, model_width):
    arrived = lax.all_to_all(
        cold_buf.reshape(experts, slot_count, model_width),
        "expert",
        split_axis=0,
        concat_axis=0,
        tiled=True,
    ).reshape(-1, model_width)
    cold_in = group_rows(arrived)
    hot_in = None
    return (cold_in, hot_in)


def return_rows(cold_part, experts, slot_count, model_width):
    cold_total = group_sum(cold_part)
    hot_out = None
    summed = cold_total.astype(jnp.bfloat16).reshape(experts, slot_count, model_width)
    cold_out = lax.all_to_all(summed, "expert", split_axis=0, concat_axis=0, tiled=True).reshape(
        -1, model_width
    )
    return (cold_out, hot_out)


def forward_rows(row_block, matrices):
    gate_up = jnp.einsum("rd,kfd->krf", row_block, matrices[:2], preferred_element_type=jnp.float32)
    gate_act = gate_up[0]
    up_act = gate_up[1]
    hidden = (gate_act * jax.nn.sigmoid(gate_act) * up_act).astype(jnp.bfloat16)
    partial_out = jnp.dot(hidden, matrices[2], preferred_element_type=jnp.float32)
    return (gate_act, up_act, partial_out)


def backward_rows(row_block, gate_act, up_act, matrices):
    hidden_grad = lax.dot_general(
        row_block, matrices[2], (((1,), (1,)), ((), ())), preferred_element_type=jnp.float32
    )
    squashed = jax.nn.sigmoid(gate_act)
    gate_grad = (hidden_grad * up_act * squashed * (1.0 + gate_act * (1.0 - squashed))).astype(
        jnp.bfloat16
    )
    up_grad = (hidden_grad * gate_act * squashed).astype(jnp.bfloat16)
    both_grads = jnp.stack([gate_grad, up_grad])
    return jnp.einsum("krf,kfd->rd", both_grads, matrices[:2], preferred_element_type=jnp.float32)


def shards(tokens, cotangent, routes, combine, expert_weights):
    weights = expert_weights[0]
    tok_dev = tokens.shape[0]
    model_width = tokens.shape[1]
    experts = lax.axis_size("expert")
    capacity = 2 * tok_dev // experts
    labels = lax.iota(jnp.int32, experts)
    member = (routes[:, None] == labels[None, :]).astype(jnp.int32)
    cold_layout = placement(member, capacity)
    cold_buf = spread(cold_layout, tokens)
    cold_in, hot_in = send_rows(cold_buf, experts, capacity, model_width)
    gate_act, up_act, cold_part = forward_rows(cold_in, weights)
    cotangent_wide = cotangent.astype(jnp.float32)
    out_grad = (combine[:, None] * cotangent_wide).astype(jnp.bfloat16)
    cold_grad_buf = spread(cold_layout, out_grad)
    cold_grad_in, hot_grad_in = send_rows(cold_grad_buf, experts, capacity, model_width)
    cold_part = cold_part.astype(jnp.bfloat16)
    cold_part, cold_grad_in = lax.optimization_barrier((cold_part, cold_grad_in))
    cold_out, hot_out = return_rows(cold_part, experts, capacity, model_width)
    expert_out = collect(cold_layout, cold_out)
    combined = (combine[:, None] * expert_out).astype(jnp.bfloat16)
    combine_grad = jnp.sum(expert_out * cotangent_wide, 1)
    cold_grad_part = backward_rows(cold_grad_in, gate_act, up_act, weights)
    cold_grad_out, hot_grad_out = return_rows(cold_grad_part, experts, capacity, model_width)
    input_grad = collect(cold_layout, cold_grad_out)
    token_grad = input_grad.astype(jnp.bfloat16)
    return (combined, token_grad, combine_grad)


def solution(mesh):
    return jax.shard_map(
        shards,
        mesh=mesh,
        in_specs=(
            P(("dp", "expert"), None),
            P(("dp", "expert"), None),
            P(("dp", "expert")),
            P(("dp", "expert")),
            P("expert", None, "dp", None),
        ),
        out_specs=(P(("dp", "expert"), None), P(("dp", "expert"), None), P(("dp", "expert"))),
        check_vma=False,
    )
```

```python
import jax
import jax.numpy as jnp
from jax import lax
from jax.sharding import PartitionSpec as P


def placement(member, slot_count):
    within = jnp.sum((jnp.cumsum(member, 0) - 1) * member, 1)
    owner_group = jnp.sum(member * lax.iota(jnp.int32, member.shape[1])[None, :], 1)
    is_used = jnp.sum(member, 1) > 0
    target = owner_group * slot_count + within
    buffer_cells = lax.iota(jnp.int32, member.shape[1] * slot_count)
    return ((buffer_cells[:, None] == target[None, :]) & is_used[None, :]).astype(jnp.bfloat16)


def spread(layout, row_block):
    return jnp.dot(layout, row_block, preferred_element_type=jnp.float32).astype(jnp.bfloat16)


def collect(layout, buffer_rows):
    return lax.dot_general(
        layout, buffer_rows, (((0,), (0,)), ((), ())), preferred_element_type=jnp.float32
    )


def shifted(values, step):
    n = lax.axis_size("dp")
    return lax.ppermute(values, "dp", perm=[(i, (i + step) % n) for i in range(n)])


def group_rows(values):
    half = values.shape[0] // 2
    from_left = shifted(values, 1)
    from_right = shifted(values, -1)
    far_head = shifted(from_left[:half], 1)
    far_tail = shifted(from_right[half:], -1)
    return jnp.concatenate([values, from_left, from_right, far_head, far_tail], 0)


def group_sum(values):
    own, to_left, to_right, far = jnp.split(values, 4, 0)
    half = far.shape[0] // 2
    far_head = shifted(far[:half].astype(jnp.bfloat16), -1).astype(jnp.float32)
    far_tail = shifted(far[half:].astype(jnp.bfloat16), 1).astype(jnp.float32)
    to_left = to_left.astype(jnp.bfloat16).astype(jnp.float32)
    to_right = to_right.astype(jnp.bfloat16).astype(jnp.float32)
    to_left = jnp.concatenate([to_left[:half] + far_head, to_left[half:]], 0)
    to_right = jnp.concatenate([to_right[:half], to_right[half:] + far_tail], 0)
    back_right = shifted(to_left.astype(jnp.bfloat16), -1).astype(jnp.float32)
    back_left = shifted(to_right.astype(jnp.bfloat16), 1).astype(jnp.float32)
    return own.astype(jnp.bfloat16).astype(jnp.float32) + back_right + back_left


def arrive_rows(cold_buf, experts, slot_count, model_width):
    return lax.all_to_all(
        cold_buf.reshape(experts, slot_count, model_width),
        "expert",
        split_axis=0,
        concat_axis=0,
        tiled=True,
    ).reshape(-1, model_width)


def return_rows(cold_part, experts, slot_count, model_width):
    cold_total = group_sum(cold_part)
    hot_out = None
    summed = cold_total.astype(jnp.bfloat16).reshape(experts, slot_count, model_width)
    cold_out = lax.all_to_all(summed, "expert", split_axis=0, concat_axis=0, tiled=True).reshape(
        -1, model_width
    )
    return (cold_out, hot_out)


def forward_rows(row_block, matrices):
    gate_up = jnp.einsum("rd,kfd->krf", row_block, matrices[:2], preferred_element_type=jnp.float32)
    gate_act = gate_up[0]
    up_act = gate_up[1]
    hidden = (gate_act * jax.nn.sigmoid(gate_act) * up_act).astype(jnp.bfloat16)
    partial_out = jnp.dot(hidden, matrices[2], preferred_element_type=jnp.float32)
    return (gate_act, up_act, partial_out)


def backward_rows(row_block, gate_act, up_act, matrices):
    hidden_grad = lax.dot_general(
        row_block, matrices[2], (((1,), (1,)), ((), ())), preferred_element_type=jnp.float32
    )
    squashed = jax.nn.sigmoid(gate_act)
    gate_grad = (hidden_grad * up_act * squashed * (1.0 + gate_act * (1.0 - squashed))).astype(
        jnp.bfloat16
    )
    up_grad = (hidden_grad * gate_act * squashed).astype(jnp.bfloat16)
    both_grads = jnp.stack([gate_grad, up_grad])
    return jnp.einsum("krf,kfd->rd", both_grads, matrices[:2], preferred_element_type=jnp.float32)


def shards(tokens, cotangent, routes, combine, expert_weights):
    weights = expert_weights[0]
    tok_dev = tokens.shape[0]
    model_width = tokens.shape[1]
    experts = lax.axis_size("expert")
    capacity = 2 * tok_dev // experts
    labels = lax.iota(jnp.int32, experts)
    member = (routes[:, None] == labels[None, :]).astype(jnp.int32)
    cold_layout = placement(member, capacity)
    cold_buf = spread(cold_layout, tokens)
    cold_in = group_rows(arrive_rows(cold_buf, experts, capacity, model_width))
    cotangent_wide = cotangent.astype(jnp.float32)
    out_grad = (combine[:, None] * cotangent_wide).astype(jnp.bfloat16)
    cold_grad_buf = spread(cold_layout, out_grad)
    cold_grad_arrived = arrive_rows(cold_grad_buf, experts, capacity, model_width)
    cold_grad_arrived, cold_in = lax.optimization_barrier((cold_grad_arrived, cold_in))
    gate_act, up_act, cold_part = forward_rows(cold_in, weights)
    cold_grad_in = group_rows(cold_grad_arrived)
    cold_part = cold_part.astype(jnp.bfloat16)
    cold_part, cold_grad_in = lax.optimization_barrier((cold_part, cold_grad_in))
    cold_out, hot_out = return_rows(cold_part, experts, capacity, model_width)
    expert_out = collect(cold_layout, cold_out)
    combined = (combine[:, None] * expert_out).astype(jnp.bfloat16)
    combine_grad = jnp.sum(expert_out * cotangent_wide, 1)
    cold_grad_part = backward_rows(cold_grad_in, gate_act, up_act, weights)
    cold_grad_out, hot_grad_out = return_rows(cold_grad_part, experts, capacity, model_width)
    input_grad = collect(cold_layout, cold_grad_out)
    token_grad = input_grad.astype(jnp.bfloat16)
    return (combined, token_grad, combine_grad)


def solution(mesh):
    return jax.shard_map(
        shards,
        mesh=mesh,
        in_specs=(
            P(("dp", "expert"), None),
            P(("dp", "expert"), None),
            P(("dp", "expert")),
            P(("dp", "expert")),
            P("expert", None, "dp", None),
        ),
        out_specs=(P(("dp", "expert"), None), P(("dp", "expert"), None), P(("dp", "expert"))),
        check_vma=False,
    )
```

```python
import jax
import jax.numpy as jnp
from jax import lax
from jax.sharding import PartitionSpec as P


def placement(member, slot_count):
    within = jnp.sum((jnp.cumsum(member, 0) - 1) * member, 1)
    owner_group = jnp.sum(member * lax.iota(jnp.int32, member.shape[1])[None, :], 1)
    is_used = jnp.sum(member, 1) > 0
    target = owner_group * slot_count + within
    buffer_cells = lax.iota(jnp.int32, member.shape[1] * slot_count)
    return ((buffer_cells[:, None] == target[None, :]) & is_used[None, :]).astype(jnp.bfloat16)


def spread(layout, row_block):
    return jnp.dot(layout, row_block, preferred_element_type=jnp.float32).astype(jnp.bfloat16)


def collect(layout, buffer_rows):
    return lax.dot_general(
        layout, buffer_rows, (((0,), (0,)), ((), ())), preferred_element_type=jnp.float32
    )


def shifted(values, step):
    n = lax.axis_size("dp")
    return lax.ppermute(values, "dp", perm=[(i, (i + step) % n) for i in range(n)])


def group_rows(values):
    half = values.shape[0] // 2
    from_left = shifted(values, 1)
    from_right = shifted(values, -1)
    far_head = shifted(from_left[:half], 1)
    far_tail = shifted(from_right[half:], -1)
    return [values, from_left, from_right, far_head, far_tail]


def sum_start(parts):
    far_head = shifted(parts[3].astype(jnp.bfloat16), -1)
    far_tail = shifted(parts[4].astype(jnp.bfloat16), 1)
    return far_head, far_tail


def sum_finish(parts, received):
    own, to_left, to_right = [p.astype(jnp.bfloat16).astype(jnp.float32) for p in parts[:3]]
    far_head, far_tail = [r.astype(jnp.float32) for r in received]
    half = far_head.shape[0]
    to_left = jnp.concatenate([to_left[:half] + far_head, to_left[half:]], 0)
    to_right = jnp.concatenate([to_right[:half], to_right[half:] + far_tail], 0)
    back_right = shifted(to_left.astype(jnp.bfloat16), -1).astype(jnp.float32)
    back_left = shifted(to_right.astype(jnp.bfloat16), 1).astype(jnp.float32)
    return own + back_right + back_left


def arrive_rows(cold_buf, experts, slot_count, model_width):
    return lax.all_to_all(
        cold_buf.reshape(experts, slot_count, model_width),
        "expert",
        split_axis=0,
        concat_axis=0,
        tiled=True,
    ).reshape(-1, model_width)


def return_rows(total, experts, slot_count, model_width):
    summed = total.astype(jnp.bfloat16).reshape(experts, slot_count, model_width)
    return lax.all_to_all(summed, "expert", split_axis=0, concat_axis=0, tiled=True).reshape(
        -1, model_width
    )


def forward_rows(row_block, matrices):
    gate_up = jnp.einsum("rd,kfd->krf", row_block, matrices[:2], preferred_element_type=jnp.float32)
    gate_act = gate_up[0]
    up_act = gate_up[1]
    hidden = (gate_act * jax.nn.sigmoid(gate_act) * up_act).astype(jnp.bfloat16)
    partial_out = jnp.dot(hidden, matrices[2], preferred_element_type=jnp.float32)
    return (gate_act, up_act, partial_out)


def backward_rows(row_block, gate_act, up_act, matrices):
    hidden_grad = lax.dot_general(
        row_block, matrices[2], (((1,), (1,)), ((), ())), preferred_element_type=jnp.float32
    )
    squashed = jax.nn.sigmoid(gate_act)
    gate_grad = (hidden_grad * up_act * squashed * (1.0 + gate_act * (1.0 - squashed))).astype(
        jnp.bfloat16
    )
    up_grad = (hidden_grad * gate_act * squashed).astype(jnp.bfloat16)
    both_grads = jnp.stack([gate_grad, up_grad])
    return jnp.einsum("krf,kfd->rd", both_grads, matrices[:2], preferred_element_type=jnp.float32)


def shards(tokens, cotangent, routes, combine, expert_weights):
    weights = expert_weights[0]
    tok_dev = tokens.shape[0]
    model_width = tokens.shape[1]
    experts = lax.axis_size("expert")
    capacity = 2 * tok_dev // experts
    labels = lax.iota(jnp.int32, experts)
    member = (routes[:, None] == labels[None, :]).astype(jnp.int32)
    cold_layout = placement(member, capacity)
    cold_buf = spread(cold_layout, tokens)
    tok_blocks = group_rows(arrive_rows(cold_buf, experts, capacity, model_width))
    cotangent_wide = cotangent.astype(jnp.float32)
    out_grad = (combine[:, None] * cotangent_wide).astype(jnp.bfloat16)
    cold_grad_buf = spread(cold_layout, out_grad)
    cold_grad_arrived = arrive_rows(cold_grad_buf, experts, capacity, model_width)
    cold_grad_arrived, tok_blocks = lax.optimization_barrier((cold_grad_arrived, tok_blocks))
    forward = [forward_rows(block, weights) for block in tok_blocks]
    fwd_parts = [f[2] for f in forward]
    cot_blocks = group_rows(cold_grad_arrived)
    fwd_received = sum_start(fwd_parts)
    fwd_received, cot_blocks = lax.optimization_barrier((fwd_received, cot_blocks))
    cold_out = return_rows(sum_finish(fwd_parts, fwd_received), experts, capacity, model_width)
    expert_out = collect(cold_layout, cold_out)
    combined = (combine[:, None] * expert_out).astype(jnp.bfloat16)
    combine_grad = jnp.sum(expert_out * cotangent_wide, 1)
    grad_parts = [
        backward_rows(block, f[0], f[1], weights) for block, f in zip(cot_blocks, forward)
    ]
    grad_total = sum_finish(grad_parts, sum_start(grad_parts))
    cold_grad_out = return_rows(grad_total, experts, capacity, model_width)
    input_grad = collect(cold_layout, cold_grad_out)
    token_grad = input_grad.astype(jnp.bfloat16)
    return (combined, token_grad, combine_grad)


def solution(mesh):
    return jax.shard_map(
        shards,
        mesh=mesh,
        in_specs=(
            P(("dp", "expert"), None),
            P(("dp", "expert"), None),
            P(("dp", "expert")),
            P(("dp", "expert")),
            P("expert", None, "dp", None),
        ),
        out_specs=(P(("dp", "expert"), None), P(("dp", "expert"), None), P(("dp", "expert"))),
        check_vma=False,
    )
```

```python
import jax
import jax.numpy as jnp
from jax import lax
from jax.sharding import PartitionSpec as P


def placement(member, slot_count):
    within = jnp.sum((jnp.cumsum(member, 0) - 1) * member, 1)
    owner_group = jnp.sum(member * lax.iota(jnp.int32, member.shape[1])[None, :], 1)
    is_used = jnp.sum(member, 1) > 0
    target = owner_group * slot_count + within
    buffer_cells = lax.iota(jnp.int32, member.shape[1] * slot_count)
    return ((buffer_cells[:, None] == target[None, :]) & is_used[None, :]).astype(jnp.bfloat16)


def spread(layout, row_block):
    return jnp.dot(layout, row_block, preferred_element_type=jnp.float32).astype(jnp.bfloat16)


def collect(layout, buffer_rows):
    return lax.dot_general(
        layout, buffer_rows, (((0,), (0,)), ((), ())), preferred_element_type=jnp.float32
    )


def shifted(values, step):
    n = lax.axis_size("dp")
    return lax.ppermute(values, "dp", perm=[(i, (i + step) % n) for i in range(n)])


def group_rows(values):
    half = values.shape[0] // 2
    from_left = shifted(values, 1)
    from_right = shifted(values, -1)
    far_head = shifted(from_left[:half], 1)
    far_tail = shifted(from_right[half:], -1)
    return [values, from_left, from_right, far_head, far_tail]


def sum_start(parts):
    far_head = shifted(parts[3].astype(jnp.bfloat16), -1)
    far_tail = shifted(parts[4].astype(jnp.bfloat16), 1)
    return far_head, far_tail


def sum_finish(parts, received):
    own, to_left, to_right = [p.astype(jnp.bfloat16).astype(jnp.float32) for p in parts[:3]]
    far_head, far_tail = [r.astype(jnp.float32) for r in received]
    half = far_head.shape[0]
    to_left = jnp.concatenate([to_left[:half] + far_head, to_left[half:]], 0)
    to_right = jnp.concatenate([to_right[:half], to_right[half:] + far_tail], 0)
    back_right = shifted(to_left.astype(jnp.bfloat16), -1).astype(jnp.float32)
    back_left = shifted(to_right.astype(jnp.bfloat16), 1).astype(jnp.float32)
    return own + back_right + back_left


def arrive_rows(cold_buf, experts, slot_count, model_width):
    return lax.all_to_all(
        cold_buf.reshape(experts, slot_count, model_width),
        "expert",
        split_axis=0,
        concat_axis=0,
        tiled=True,
    ).reshape(-1, model_width)


def return_rows(total, experts, slot_count, model_width):
    summed = total.astype(jnp.bfloat16).reshape(experts, slot_count, model_width)
    return lax.all_to_all(summed, "expert", split_axis=0, concat_axis=0, tiled=True).reshape(
        -1, model_width
    )


def forward_rows(row_block, matrices):
    gate_up = jnp.einsum("rd,kfd->krf", row_block, matrices[:2], preferred_element_type=jnp.float32)
    gate_act = gate_up[0]
    up_act = gate_up[1]
    hidden = (gate_act * jax.nn.sigmoid(gate_act) * up_act).astype(jnp.bfloat16)
    partial_out = jnp.dot(hidden, matrices[2], preferred_element_type=jnp.float32)
    return (gate_act, up_act, partial_out)


def backward_rows(row_block, gate_act, up_act, matrices):
    hidden_grad = lax.dot_general(
        row_block, matrices[2], (((1,), (1,)), ((), ())), preferred_element_type=jnp.float32
    )
    squashed = jax.nn.sigmoid(gate_act)
    gate_grad = (hidden_grad * up_act * squashed * (1.0 + gate_act * (1.0 - squashed))).astype(
        jnp.bfloat16
    )
    up_grad = (hidden_grad * gate_act * squashed).astype(jnp.bfloat16)
    both_grads = jnp.stack([gate_grad, up_grad])
    return jnp.einsum("krf,kfd->rd", both_grads, matrices[:2], preferred_element_type=jnp.float32)


def shards(tokens, cotangent, routes, combine, expert_weights):
    weights = expert_weights[0]
    tok_dev = tokens.shape[0]
    model_width = tokens.shape[1]
    experts = lax.axis_size("expert")
    capacity = 2 * tok_dev // experts
    pieces = 2
    piece_slots = capacity // pieces
    labels = lax.iota(jnp.int32, experts)
    member = (routes[:, None] == labels[None, :]).astype(jnp.int32)
    cold_layout = placement(member, capacity).reshape(experts, capacity, tok_dev)
    layouts = [
        cold_layout[:, k * piece_slots:(k + 1) * piece_slots].reshape(-1, tok_dev)
        for k in range(pieces)
    ]
    tok_arrived = [
        arrive_rows(spread(lay, tokens), experts, piece_slots, model_width) for lay in layouts
    ]
    tok_blocks = [group_rows(arr) for arr in tok_arrived]
    cotangent_wide = cotangent.astype(jnp.float32)
    out_grad = (combine[:, None] * cotangent_wide).astype(jnp.bfloat16)
    cot_arrived = [
        arrive_rows(spread(lay, out_grad), experts, piece_slots, model_width) for lay in layouts
    ]
    cot_arrived, tok_blocks = lax.optimization_barrier((cot_arrived, tok_blocks))
    forward = [[forward_rows(block, weights) for block in blocks] for blocks in tok_blocks]
    fwd_parts = [[f[2] for f in fw] for fw in forward]
    cot_blocks = [group_rows(arr) for arr in cot_arrived]
    fwd_received = [sum_start(parts) for parts in fwd_parts]
    fwd_received, cot_blocks = lax.optimization_barrier((fwd_received, cot_blocks))
    expert_out = None
    for lay, parts, received in zip(layouts, fwd_parts, fwd_received):
        back = return_rows(sum_finish(parts, received), experts, piece_slots, model_width)
        piece = collect(lay, back)
        expert_out = piece if expert_out is None else expert_out + piece
    combined = (combine[:, None] * expert_out).astype(jnp.bfloat16)
    combine_grad = jnp.sum(expert_out * cotangent_wide, 1)
    input_grad = None
    for lay, blocks, fw in zip(layouts, cot_blocks, forward):
        grad_parts = [backward_rows(block, f[0], f[1], weights) for block, f in zip(blocks, fw)]
        grad_total = sum_finish(grad_parts, sum_start(grad_parts))
        back = return_rows(grad_total, experts, piece_slots, model_width)
        piece = collect(lay, back)
        input_grad = piece if input_grad is None else input_grad + piece
    token_grad = input_grad.astype(jnp.bfloat16)
    return (combined, token_grad, combine_grad)


def solution(mesh):
    return jax.shard_map(
        shards,
        mesh=mesh,
        in_specs=(
            P(("dp", "expert"), None),
            P(("dp", "expert"), None),
            P(("dp", "expert")),
            P(("dp", "expert")),
            P("expert", None, "dp", None),
        ),
        out_specs=(P(("dp", "expert"), None), P(("dp", "expert"), None), P(("dp", "expert"))),
        check_vma=False,
    )
```

```python
import jax
import jax.numpy as jnp
from jax import lax
from jax.sharding import PartitionSpec as P


def placement(member, slot_count):
    within = jnp.sum((jnp.cumsum(member, 0) - 1) * member, 1)
    owner_group = jnp.sum(member * lax.iota(jnp.int32, member.shape[1])[None, :], 1)
    is_used = jnp.sum(member, 1) > 0
    target = owner_group * slot_count + within
    buffer_cells = lax.iota(jnp.int32, member.shape[1] * slot_count)
    return ((buffer_cells[:, None] == target[None, :]) & is_used[None, :]).astype(jnp.bfloat16)


def spread(layout, row_block):
    return jnp.dot(layout, row_block, preferred_element_type=jnp.float32).astype(jnp.bfloat16)


def collect(layout, buffer_rows):
    return lax.dot_general(
        layout, buffer_rows, (((0,), (0,)), ((), ())), preferred_element_type=jnp.float32
    )


def shifted(values, step):
    n = lax.axis_size("dp")
    return lax.ppermute(values, "dp", perm=[(i, (i + step) % n) for i in range(n)])


def group_rows(values):
    half = values.shape[0] // 2
    left_lo = shifted(values[:half], 1)
    right_hi = shifted(values[half:], -1)
    far_head = shifted(left_lo, 1)
    far_tail = shifted(right_hi, -1)
    left_hi = shifted(values[half:], 1)
    right_lo = shifted(values[:half], -1)
    return [values, left_lo, left_hi, right_lo, right_hi, far_head, far_tail]


def sum_start(parts):
    far_head = shifted(parts[5].astype(jnp.bfloat16), -1)
    far_tail = shifted(parts[6].astype(jnp.bfloat16), 1)
    return far_head, far_tail


def sum_finish(parts, received):
    own, left_lo, left_hi, right_lo, right_hi = parts[:5]
    far_head, far_tail = [r.astype(jnp.float32) for r in received]

    def wide(x):
        return x.astype(jnp.bfloat16).astype(jnp.float32)

    back_hi_a = shifted(left_hi.astype(jnp.bfloat16), -1).astype(jnp.float32)
    back_lo_b = shifted(right_lo.astype(jnp.bfloat16), 1).astype(jnp.float32)
    back_lo_a = shifted((wide(left_lo) + far_head).astype(jnp.bfloat16), -1).astype(jnp.float32)
    back_hi_b = shifted((wide(right_hi) + far_tail).astype(jnp.bfloat16), 1).astype(jnp.float32)
    return wide(own) + jnp.concatenate([back_lo_a + back_lo_b, back_hi_a + back_hi_b], 0)


def arrive_rows(cold_buf, experts, slot_count, model_width):
    return lax.all_to_all(
        cold_buf.reshape(experts, slot_count, model_width),
        "expert",
        split_axis=0,
        concat_axis=0,
        tiled=True,
    ).reshape(-1, model_width)


def return_rows(total, experts, slot_count, model_width):
    summed = total.astype(jnp.bfloat16).reshape(experts, slot_count, model_width)
    return lax.all_to_all(summed, "expert", split_axis=0, concat_axis=0, tiled=True).reshape(
        -1, model_width
    )


def forward_rows(row_block, matrices):
    gate_up = jnp.einsum("rd,kfd->krf", row_block, matrices[:2], preferred_element_type=jnp.float32)
    gate_act = gate_up[0]
    up_act = gate_up[1]
    hidden = (gate_act * jax.nn.sigmoid(gate_act) * up_act).astype(jnp.bfloat16)
    partial_out = jnp.dot(hidden, matrices[2], preferred_element_type=jnp.float32)
    return (gate_act, up_act, partial_out)


def backward_rows(row_block, gate_act, up_act, matrices):
    hidden_grad = lax.dot_general(
        row_block, matrices[2], (((1,), (1,)), ((), ())), preferred_element_type=jnp.float32
    )
    squashed = jax.nn.sigmoid(gate_act)
    gate_grad = (hidden_grad * up_act * squashed * (1.0 + gate_act * (1.0 - squashed))).astype(
        jnp.bfloat16
    )
    up_grad = (hidden_grad * gate_act * squashed).astype(jnp.bfloat16)
    both_grads = jnp.stack([gate_grad, up_grad])
    return jnp.einsum("krf,kfd->rd", both_grads, matrices[:2], preferred_element_type=jnp.float32)


def shards(tokens, cotangent, routes, combine, expert_weights):
    weights = expert_weights[0]
    tok_dev = tokens.shape[0]
    model_width = tokens.shape[1]
    experts = lax.axis_size("expert")
    capacity = 2 * tok_dev // experts
    labels = lax.iota(jnp.int32, experts)
    member = (routes[:, None] == labels[None, :]).astype(jnp.int32)
    cold_layout = placement(member, capacity)
    cold_buf = spread(cold_layout, tokens)
    tok_blocks = group_rows(arrive_rows(cold_buf, experts, capacity, model_width))
    cotangent_wide = cotangent.astype(jnp.float32)
    out_grad = (combine[:, None] * cotangent_wide).astype(jnp.bfloat16)
    cold_grad_buf = spread(cold_layout, out_grad)
    cold_grad_arrived = arrive_rows(cold_grad_buf, experts, capacity, model_width)
    cold_grad_arrived, tok_blocks = lax.optimization_barrier((cold_grad_arrived, tok_blocks))
    forward = [forward_rows(block, weights) for block in tok_blocks]
    fwd_parts = [f[2] for f in forward]
    cot_blocks = group_rows(cold_grad_arrived)
    fwd_received = sum_start(fwd_parts)
    fwd_received, cot_blocks = lax.optimization_barrier((fwd_received, cot_blocks))
    cold_out = return_rows(sum_finish(fwd_parts, fwd_received), experts, capacity, model_width)
    expert_out = collect(cold_layout, cold_out)
    combined = (combine[:, None] * expert_out).astype(jnp.bfloat16)
    combine_grad = jnp.sum(expert_out * cotangent_wide, 1)
    grad_parts = [
        backward_rows(block, f[0], f[1], weights) for block, f in zip(cot_blocks, forward)
    ]
    grad_total = sum_finish(grad_parts, sum_start(grad_parts))
    cold_grad_out = return_rows(grad_total, experts, capacity, model_width)
    input_grad = collect(cold_layout, cold_grad_out)
    token_grad = input_grad.astype(jnp.bfloat16)
    return (combined, token_grad, combine_grad)


def solution(mesh):
    return jax.shard_map(
        shards,
        mesh=mesh,
        in_specs=(
            P(("dp", "expert"), None),
            P(("dp", "expert"), None),
            P(("dp", "expert")),
            P(("dp", "expert")),
            P("expert", None, "dp", None),
        ),
        out_specs=(P(("dp", "expert"), None), P(("dp", "expert"), None), P(("dp", "expert"))),
        check_vma=False,
    )
```

```python
import jax
import jax.numpy as jnp
from jax import lax
from jax.sharding import PartitionSpec as P


def placement(member, slot_count):
    within = jnp.sum((jnp.cumsum(member, 0) - 1) * member, 1)
    owner_group = jnp.sum(member * lax.iota(jnp.int32, member.shape[1])[None, :], 1)
    is_used = jnp.sum(member, 1) > 0
    target = owner_group * slot_count + within
    buffer_cells = lax.iota(jnp.int32, member.shape[1] * slot_count)
    return ((buffer_cells[:, None] == target[None, :]) & is_used[None, :]).astype(jnp.bfloat16)


def spread(layout, row_block):
    return jnp.dot(layout, row_block, preferred_element_type=jnp.float32).astype(jnp.bfloat16)


def collect(layout, buffer_rows):
    return lax.dot_general(
        layout, buffer_rows, (((0,), (0,)), ((), ())), preferred_element_type=jnp.float32
    )


def shifted(values, step):
    n = lax.axis_size("dp")
    return lax.ppermute(values, "dp", perm=[(i, (i + step) % n) for i in range(n)])


def group_rows(values):
    half = values.shape[0] // 2
    left_lo = shifted(values[:half], 1)
    right_hi = shifted(values[half:], -1)
    far_head = shifted(left_lo, 1)
    far_tail = shifted(right_hi, -1)
    left_hi = shifted(values[half:], 1)
    right_lo = shifted(values[:half], -1)
    return [values, left_lo, left_hi, right_lo, right_hi, far_head, far_tail]


def sum_start(parts):
    far_head = shifted(parts[5].astype(jnp.bfloat16), -1)
    far_tail = shifted(parts[6].astype(jnp.bfloat16), 1)
    return far_head, far_tail


def sum_finish(parts, received):
    own, left_lo, left_hi, right_lo, right_hi = parts[:5]
    far_head, far_tail = [r.astype(jnp.float32) for r in received]

    def wide(x):
        return x.astype(jnp.bfloat16).astype(jnp.float32)

    back_hi_a = shifted(left_hi.astype(jnp.bfloat16), -1).astype(jnp.float32)
    back_lo_b = shifted(right_lo.astype(jnp.bfloat16), 1).astype(jnp.float32)
    back_lo_a = shifted((wide(left_lo) + far_head).astype(jnp.bfloat16), -1).astype(jnp.float32)
    back_hi_b = shifted((wide(right_hi) + far_tail).astype(jnp.bfloat16), 1).astype(jnp.float32)
    return wide(own) + jnp.concatenate([back_lo_a + back_lo_b, back_hi_a + back_hi_b], 0)


def arrive_rows(cold_buf, experts, slot_count, model_width):
    return lax.all_to_all(
        cold_buf.reshape(experts, slot_count, model_width),
        "expert",
        split_axis=0,
        concat_axis=0,
        tiled=True,
    ).reshape(-1, model_width)


def return_rows(total, experts, slot_count, model_width):
    summed = total.astype(jnp.bfloat16).reshape(experts, slot_count, model_width)
    return lax.all_to_all(summed, "expert", split_axis=0, concat_axis=0, tiled=True).reshape(
        -1, model_width
    )


def forward_rows(row_block, matrices):
    gate_up = jnp.einsum("rd,kfd->krf", row_block, matrices[:2], preferred_element_type=jnp.float32)
    gate_act = gate_up[0]
    up_act = gate_up[1]
    hidden = (gate_act * jax.nn.sigmoid(gate_act) * up_act).astype(jnp.bfloat16)
    partial_out = jnp.dot(hidden, matrices[2], preferred_element_type=jnp.float32)
    return (gate_act, up_act, partial_out)


def backward_rows(row_block, gate_act, up_act, matrices):
    hidden_grad = lax.dot_general(
        row_block, matrices[2], (((1,), (1,)), ((), ())), preferred_element_type=jnp.float32
    )
    squashed = jax.nn.sigmoid(gate_act)
    gate_grad = (hidden_grad * up_act * squashed * (1.0 + gate_act * (1.0 - squashed))).astype(
        jnp.bfloat16
    )
    up_grad = (hidden_grad * gate_act * squashed).astype(jnp.bfloat16)
    both_grads = jnp.stack([gate_grad, up_grad])
    return jnp.einsum("krf,kfd->rd", both_grads, matrices[:2], preferred_element_type=jnp.float32)


def shards(tokens, cotangent, routes, combine, expert_weights):
    weights = expert_weights[0]
    tok_dev = tokens.shape[0]
    model_width = tokens.shape[1]
    experts = lax.axis_size("expert")
    capacity = 2 * tok_dev // experts
    labels = lax.iota(jnp.int32, experts)
    member = (routes[:, None] == labels[None, :]).astype(jnp.int32)
    cold_layout = placement(member, capacity)
    cold_buf = spread(cold_layout, tokens)
    tok_blocks = group_rows(arrive_rows(cold_buf, experts, capacity, model_width))
    cotangent_wide = cotangent.astype(jnp.float32)
    out_grad = (combine[:, None] * cotangent_wide).astype(jnp.bfloat16)
    cold_grad_buf = spread(cold_layout, out_grad)
    cold_grad_arrived = arrive_rows(cold_grad_buf, experts, capacity, model_width)
    cold_grad_arrived, tok_blocks = lax.optimization_barrier((cold_grad_arrived, tok_blocks))
    forward = [forward_rows(block, weights) for block in tok_blocks]
    fwd_parts = [f[2] for f in forward]
    cot_blocks = group_rows(cold_grad_arrived)
    fwd_received = sum_start(fwd_parts)
    fwd_received, cot_blocks = lax.optimization_barrier((fwd_received, cot_blocks))
    fwd_total = sum_finish(fwd_parts, fwd_received)
    grad_parts = [
        backward_rows(block, f[0], f[1], weights) for block, f in zip(cot_blocks, forward)
    ]
    fwd_total, grad_parts = lax.optimization_barrier((fwd_total, grad_parts))
    cold_out = return_rows(fwd_total, experts, capacity, model_width)
    expert_out = collect(cold_layout, cold_out)
    combined = (combine[:, None] * expert_out).astype(jnp.bfloat16)
    combine_grad = jnp.sum(expert_out * cotangent_wide, 1)
    grad_total = sum_finish(grad_parts, sum_start(grad_parts))
    cold_grad_out = return_rows(grad_total, experts, capacity, model_width)
    input_grad = collect(cold_layout, cold_grad_out)
    token_grad = input_grad.astype(jnp.bfloat16)
    return (combined, token_grad, combine_grad)


def solution(mesh):
    return jax.shard_map(
        shards,
        mesh=mesh,
        in_specs=(
            P(("dp", "expert"), None),
            P(("dp", "expert"), None),
            P(("dp", "expert")),
            P(("dp", "expert")),
            P("expert", None, "dp", None),
        ),
        out_specs=(P(("dp", "expert"), None), P(("dp", "expert"), None), P(("dp", "expert"))),
        check_vma=False,
    )
```

```python
import jax
import jax.numpy as jnp
from jax import lax
from jax.sharding import PartitionSpec as P


def placement(member, slot_count):
    within = jnp.sum((jnp.cumsum(member, 0) - 1) * member, 1)
    owner_group = jnp.sum(member * lax.iota(jnp.int32, member.shape[1])[None, :], 1)
    is_used = jnp.sum(member, 1) > 0
    target = owner_group * slot_count + within
    buffer_cells = lax.iota(jnp.int32, member.shape[1] * slot_count)
    return ((buffer_cells[:, None] == target[None, :]) & is_used[None, :]).astype(jnp.bfloat16)


def spread(layout, row_block):
    return jnp.dot(layout, row_block, preferred_element_type=jnp.float32).astype(jnp.bfloat16)


def collect(layout, buffer_rows):
    return lax.dot_general(
        layout, buffer_rows, (((0,), (0,)), ((), ())), preferred_element_type=jnp.float32
    )


def shifted(values, step):
    n = lax.axis_size("dp")
    return lax.ppermute(values, "dp", perm=[(i, (i + step) % n) for i in range(n)])


def group_rows(values):
    half = values.shape[0] // 2
    left_lo = shifted(values[:half], 1)
    right_hi = shifted(values[half:], -1)
    far_head = shifted(left_lo, 1)
    far_tail = shifted(right_hi, -1)
    left_hi = shifted(values[half:], 1)
    right_lo = shifted(values[:half], -1)
    return [values, left_lo, left_hi, right_lo, right_hi, far_head, far_tail]


def sum_start(parts):
    far_head = shifted(parts[5].astype(jnp.bfloat16), -1)
    far_tail = shifted(parts[6].astype(jnp.bfloat16), 1)
    return far_head, far_tail


def sum_finish(parts, received):
    own, left_lo, left_hi, right_lo, right_hi = parts[:5]
    far_head, far_tail = [r.astype(jnp.float32) for r in received]

    def wide(x):
        return x.astype(jnp.bfloat16).astype(jnp.float32)

    back_hi_a = shifted(left_hi.astype(jnp.bfloat16), -1).astype(jnp.float32)
    back_lo_b = shifted(right_lo.astype(jnp.bfloat16), 1).astype(jnp.float32)
    back_lo_a = shifted((wide(left_lo) + far_head).astype(jnp.bfloat16), -1).astype(jnp.float32)
    back_hi_b = shifted((wide(right_hi) + far_tail).astype(jnp.bfloat16), 1).astype(jnp.float32)
    return wide(own) + jnp.concatenate([back_lo_a + back_lo_b, back_hi_a + back_hi_b], 0)


def arrive_rows(cold_buf, experts, slot_count, model_width):
    return lax.all_to_all(
        cold_buf.reshape(experts, slot_count, model_width),
        "expert",
        split_axis=0,
        concat_axis=0,
        tiled=True,
    ).reshape(-1, model_width)


def return_rows(total, experts, slot_count, model_width):
    summed = total.astype(jnp.bfloat16).reshape(experts, slot_count, model_width)
    return lax.all_to_all(summed, "expert", split_axis=0, concat_axis=0, tiled=True).reshape(
        -1, model_width
    )


def forward_rows(row_block, matrices):
    gate_up = jnp.einsum("rd,kfd->krf", row_block, matrices[:2], preferred_element_type=jnp.float32)
    gate_act = gate_up[0]
    up_act = gate_up[1]
    hidden = (gate_act * jax.nn.sigmoid(gate_act) * up_act).astype(jnp.bfloat16)
    partial_out = jnp.dot(hidden, matrices[2], preferred_element_type=jnp.float32)
    return (gate_act, up_act, partial_out)


def backward_rows(row_block, gate_act, up_act, matrices):
    hidden_grad = lax.dot_general(
        row_block, matrices[2], (((1,), (1,)), ((), ())), preferred_element_type=jnp.float32
    )
    squashed = jax.nn.sigmoid(gate_act)
    gate_grad = (hidden_grad * up_act * squashed * (1.0 + gate_act * (1.0 - squashed))).astype(
        jnp.bfloat16
    )
    up_grad = (hidden_grad * gate_act * squashed).astype(jnp.bfloat16)
    both_grads = jnp.stack([gate_grad, up_grad])
    return jnp.einsum("krf,kfd->rd", both_grads, matrices[:2], preferred_element_type=jnp.float32)


def shards(tokens, cotangent, routes, combine, expert_weights):
    weights = expert_weights[0]
    tok_dev = tokens.shape[0]
    model_width = tokens.shape[1]
    experts = lax.axis_size("expert")
    capacity = 2 * tok_dev // experts
    labels = lax.iota(jnp.int32, experts)
    member = (routes[:, None] == labels[None, :]).astype(jnp.int32)
    cold_layout = placement(member, capacity)
    cold_buf = spread(cold_layout, tokens)
    tok_blocks = group_rows(arrive_rows(cold_buf, experts, capacity, model_width))
    cotangent_wide = cotangent.astype(jnp.float32)
    out_grad = (combine[:, None] * cotangent_wide).astype(jnp.bfloat16)
    cold_grad_buf = spread(cold_layout, out_grad)
    cold_grad_buf, tok_blocks[1] = lax.optimization_barrier((cold_grad_buf, tok_blocks[1]))
    cold_grad_arrived = arrive_rows(cold_grad_buf, experts, capacity, model_width)
    cold_grad_arrived, tok_blocks[:5] = lax.optimization_barrier(
        (cold_grad_arrived, tok_blocks[:5])
    )
    forward = [forward_rows(block, weights) for block in tok_blocks]
    fwd_parts = [f[2] for f in forward]
    cot_blocks = group_rows(cold_grad_arrived)
    fwd_received = sum_start(fwd_parts)
    fwd_received, cot_blocks = lax.optimization_barrier((fwd_received, cot_blocks))
    fwd_total = sum_finish(fwd_parts, fwd_received)
    grad_parts = [
        backward_rows(block, f[0], f[1], weights) for block, f in zip(cot_blocks, forward)
    ]
    fwd_total, grad_parts = lax.optimization_barrier((fwd_total, grad_parts))
    cold_out = return_rows(fwd_total, experts, capacity, model_width)
    expert_out = collect(cold_layout, cold_out)
    combined = (combine[:, None] * expert_out).astype(jnp.bfloat16)
    combine_grad = jnp.sum(expert_out * cotangent_wide, 1)
    grad_total = sum_finish(grad_parts, sum_start(grad_parts))
    cold_grad_out = return_rows(grad_total, experts, capacity, model_width)
    input_grad = collect(cold_layout, cold_grad_out)
    token_grad = input_grad.astype(jnp.bfloat16)
    return (combined, token_grad, combine_grad)


def solution(mesh):
    return jax.shard_map(
        shards,
        mesh=mesh,
        in_specs=(
            P(("dp", "expert"), None),
            P(("dp", "expert"), None),
            P(("dp", "expert")),
            P(("dp", "expert")),
            P("expert", None, "dp", None),
        ),
        out_specs=(P(("dp", "expert"), None), P(("dp", "expert"), None), P(("dp", "expert"))),
        check_vma=False,
    )
```

```python
import jax
import jax.numpy as jnp
from jax import lax
from jax.sharding import PartitionSpec as P


def placement(member, slot_count):
    within = jnp.sum((jnp.cumsum(member, 0) - 1) * member, 1)
    owner_group = jnp.sum(member * lax.iota(jnp.int32, member.shape[1])[None, :], 1)
    is_used = jnp.sum(member, 1) > 0
    target = owner_group * slot_count + within
    buffer_cells = lax.iota(jnp.int32, member.shape[1] * slot_count)
    return ((buffer_cells[:, None] == target[None, :]) & is_used[None, :]).astype(jnp.bfloat16)


def spread(layout, row_block):
    return jnp.dot(layout, row_block, preferred_element_type=jnp.float32).astype(jnp.bfloat16)


def collect(layout, buffer_rows):
    return lax.dot_general(
        layout, buffer_rows, (((0,), (0,)), ((), ())), preferred_element_type=jnp.float32
    )


def shifted(values, step):
    n = lax.axis_size("dp")
    return lax.ppermute(values, "dp", perm=[(i, (i + step) % n) for i in range(n)])


def group_rows(values):
    half = values.shape[0] // 2
    left_lo = shifted(values[:half], 1)
    right_hi = shifted(values[half:], -1)
    far_head = shifted(left_lo, 1)
    far_tail = shifted(right_hi, -1)
    left_hi = shifted(values[half:], 1)
    right_lo = shifted(values[:half], -1)
    return [values, left_lo, left_hi, right_lo, right_hi, far_head, far_tail]


def sum_start(parts):
    far_head = shifted(parts[5].astype(jnp.bfloat16), -1)
    far_tail = shifted(parts[6].astype(jnp.bfloat16), 1)
    return far_head, far_tail


def sum_finish(parts, received):
    own, left_lo, left_hi, right_lo, right_hi = parts[:5]
    far_head, far_tail = [r.astype(jnp.float32) for r in received]

    def wide(x):
        return x.astype(jnp.bfloat16).astype(jnp.float32)

    back_hi_a = shifted(left_hi.astype(jnp.bfloat16), -1).astype(jnp.float32)
    back_lo_b = shifted(right_lo.astype(jnp.bfloat16), 1).astype(jnp.float32)
    back_lo_a = shifted((wide(left_lo) + far_head).astype(jnp.bfloat16), -1).astype(jnp.float32)
    back_hi_b = shifted((wide(right_hi) + far_tail).astype(jnp.bfloat16), 1).astype(jnp.float32)
    return wide(own) + jnp.concatenate([back_lo_a + back_lo_b, back_hi_a + back_hi_b], 0)


def arrive_rows(cold_buf, experts, slot_count, model_width):
    return lax.all_to_all(
        cold_buf.reshape(experts, slot_count, model_width),
        "expert",
        split_axis=0,
        concat_axis=0,
        tiled=True,
    ).reshape(-1, model_width)


def return_rows(total, experts, slot_count, model_width):
    summed = total.astype(jnp.bfloat16).reshape(experts, slot_count, model_width)
    return lax.all_to_all(summed, "expert", split_axis=0, concat_axis=0, tiled=True).reshape(
        -1, model_width
    )


def forward_rows(row_block, matrices):
    gate_up = jnp.einsum("rd,kfd->krf", row_block, matrices[:2], preferred_element_type=jnp.float32)
    gate_act = gate_up[0]
    up_act = gate_up[1]
    hidden = (gate_act * jax.nn.sigmoid(gate_act) * up_act).astype(jnp.bfloat16)
    partial_out = jnp.dot(hidden, matrices[2], preferred_element_type=jnp.float32)
    return (gate_act, up_act, partial_out)


def backward_rows(row_block, gate_act, up_act, matrices):
    hidden_grad = lax.dot_general(
        row_block, matrices[2], (((1,), (1,)), ((), ())), preferred_element_type=jnp.float32
    )
    squashed = jax.nn.sigmoid(gate_act)
    gate_grad = (hidden_grad * up_act * squashed * (1.0 + gate_act * (1.0 - squashed))).astype(
        jnp.bfloat16
    )
    up_grad = (hidden_grad * gate_act * squashed).astype(jnp.bfloat16)
    both_grads = jnp.stack([gate_grad, up_grad])
    return jnp.einsum("krf,kfd->rd", both_grads, matrices[:2], preferred_element_type=jnp.float32)


def shards(tokens, cotangent, routes, combine, expert_weights):
    weights = expert_weights[0]
    tok_dev = tokens.shape[0]
    model_width = tokens.shape[1]
    experts = lax.axis_size("expert")
    capacity = 2 * tok_dev // experts
    labels = lax.iota(jnp.int32, experts)
    member = (routes[:, None] == labels[None, :]).astype(jnp.int32)
    cold_layout = placement(member, capacity)
    cold_buf = spread(cold_layout, tokens)
    tok_blocks = group_rows(arrive_rows(cold_buf, experts, capacity, model_width))
    cotangent_wide = cotangent.astype(jnp.float32)
    out_grad = (combine[:, None] * cotangent_wide).astype(jnp.bfloat16)
    cold_grad_buf = spread(cold_layout, out_grad)
    cold_grad_arrived = arrive_rows(cold_grad_buf, experts, capacity, model_width)
    cold_grad_arrived, tok_blocks[:5] = lax.optimization_barrier(
        (cold_grad_arrived, tok_blocks[:5])
    )
    forward = [forward_rows(block, weights) for block in tok_blocks]
    fwd_parts = [f[2] for f in forward]
    cot_blocks = group_rows(cold_grad_arrived)
    fwd_received = sum_start(fwd_parts)
    fwd_received, cot_blocks = lax.optimization_barrier((fwd_received, cot_blocks))
    fwd_total = sum_finish(fwd_parts, fwd_received)
    grad_parts = [
        backward_rows(block, f[0], f[1], weights) for block, f in zip(cot_blocks, forward)
    ]
    fwd_total, grad_parts = lax.optimization_barrier((fwd_total, grad_parts))
    cold_out = return_rows(fwd_total, experts, capacity, model_width)
    expert_out = collect(cold_layout, cold_out)
    combined = (combine[:, None] * expert_out).astype(jnp.bfloat16)
    combine_grad = jnp.sum(expert_out * cotangent_wide, 1)
    grad_total = sum_finish(grad_parts, sum_start(grad_parts))
    cold_grad_out = return_rows(grad_total, experts, capacity, model_width)
    input_grad = collect(cold_layout, cold_grad_out)
    token_grad = input_grad.astype(jnp.bfloat16)
    return (combined, token_grad, combine_grad)


def solution(mesh):
    return jax.shard_map(
        shards,
        mesh=mesh,
        in_specs=(
            P(("dp", "expert"), None),
            P(("dp", "expert"), None),
            P(("dp", "expert")),
            P(("dp", "expert")),
            P("expert", None, "dp", None),
        ),
        out_specs=(P(("dp", "expert"), None), P(("dp", "expert"), None), P(("dp", "expert"))),
        check_vma=False,
    )
```

```python
import jax
import jax.numpy as jnp
from jax import lax
from jax.sharding import PartitionSpec as P


def placement(member, slot_count):
    within = jnp.sum((jnp.cumsum(member, 0) - 1) * member, 1)
    owner_group = jnp.sum(member * lax.iota(jnp.int32, member.shape[1])[None, :], 1)
    is_used = jnp.sum(member, 1) > 0
    target = owner_group * slot_count + within
    buffer_cells = lax.iota(jnp.int32, member.shape[1] * slot_count)
    return ((buffer_cells[:, None] == target[None, :]) & is_used[None, :]).astype(jnp.bfloat16)


def spread(layout, row_block):
    return jnp.dot(layout, row_block, preferred_element_type=jnp.float32).astype(jnp.bfloat16)


def collect(layout, buffer_rows):
    return lax.dot_general(
        layout, buffer_rows, (((0,), (0,)), ((), ())), preferred_element_type=jnp.float32
    )


def shifted(values, step):
    n = lax.axis_size("dp")
    return lax.ppermute(values, "dp", perm=[(i, (i + step) % n) for i in range(n)])


def group_rows(lo, hi):
    left_lo = shifted(lo, 1)
    right_lo = shifted(lo, -1)
    far_head = shifted(left_lo, 1)
    right_hi = shifted(hi, -1)
    left_hi = shifted(hi, 1)
    far_tail = shifted(right_hi, -1)
    return [lo, hi, left_lo, left_hi, right_lo, right_hi, far_head, far_tail]


def sum_start(parts):
    far_head = shifted(parts[6].astype(jnp.bfloat16), -1)
    far_tail = shifted(parts[7].astype(jnp.bfloat16), 1)
    return far_head, far_tail


def sum_finish(parts, received):
    own_lo, own_hi, left_lo, left_hi, right_lo, right_hi = parts[:6]
    far_head, far_tail = [r.astype(jnp.float32) for r in received]

    def wide(x):
        return x.astype(jnp.bfloat16).astype(jnp.float32)

    back_lo_b = shifted(right_lo.astype(jnp.bfloat16), 1).astype(jnp.float32)
    back_lo_a = shifted((wide(left_lo) + far_head).astype(jnp.bfloat16), -1).astype(jnp.float32)
    back_hi_a = shifted(left_hi.astype(jnp.bfloat16), -1).astype(jnp.float32)
    back_hi_b = shifted((wide(right_hi) + far_tail).astype(jnp.bfloat16), 1).astype(jnp.float32)
    return wide(own_lo) + back_lo_a + back_lo_b, wide(own_hi) + back_hi_a + back_hi_b


def arrive_rows(cold_buf, experts, slot_count, model_width):
    return lax.all_to_all(
        cold_buf.reshape(experts, slot_count, model_width),
        "expert",
        split_axis=0,
        concat_axis=0,
        tiled=True,
    ).reshape(-1, model_width)


def return_rows(total, experts, slot_count, model_width):
    summed = total.astype(jnp.bfloat16).reshape(experts, slot_count, model_width)
    return lax.all_to_all(summed, "expert", split_axis=0, concat_axis=0, tiled=True).reshape(
        -1, model_width
    )


def forward_rows(row_block, matrices):
    gate_up = jnp.einsum("rd,kfd->krf", row_block, matrices[:2], preferred_element_type=jnp.float32)
    gate_act = gate_up[0]
    up_act = gate_up[1]
    hidden = (gate_act * jax.nn.sigmoid(gate_act) * up_act).astype(jnp.bfloat16)
    partial_out = jnp.dot(hidden, matrices[2], preferred_element_type=jnp.float32)
    return (gate_act, up_act, partial_out)


def backward_rows(row_block, gate_act, up_act, matrices):
    hidden_grad = lax.dot_general(
        row_block, matrices[2], (((1,), (1,)), ((), ())), preferred_element_type=jnp.float32
    )
    squashed = jax.nn.sigmoid(gate_act)
    gate_grad = (hidden_grad * up_act * squashed * (1.0 + gate_act * (1.0 - squashed))).astype(
        jnp.bfloat16
    )
    up_grad = (hidden_grad * gate_act * squashed).astype(jnp.bfloat16)
    both_grads = jnp.stack([gate_grad, up_grad])
    return jnp.einsum("krf,kfd->rd", both_grads, matrices[:2], preferred_element_type=jnp.float32)


def shards(tokens, cotangent, routes, combine, expert_weights):
    weights = expert_weights[0]
    tok_dev = tokens.shape[0]
    model_width = tokens.shape[1]
    experts = lax.axis_size("expert")
    capacity = 2 * tok_dev // experts
    half_slots = capacity // 2
    labels = lax.iota(jnp.int32, experts)
    member = (routes[:, None] == labels[None, :]).astype(jnp.int32)
    cold_layout = placement(member, capacity).reshape(experts, capacity, tok_dev)
    layout_lo = cold_layout[:, :half_slots].reshape(-1, tok_dev)
    layout_hi = cold_layout[:, half_slots:].reshape(-1, tok_dev)

    def arrive(layout, rows):
        return arrive_rows(spread(layout, rows), experts, half_slots, model_width)

    tok_lo = arrive(layout_lo, tokens)
    tok_hi = arrive(layout_hi, tokens)
    tok_blocks = group_rows(tok_lo, tok_hi)
    cotangent_wide = cotangent.astype(jnp.float32)
    out_grad = (combine[:, None] * cotangent_wide).astype(jnp.bfloat16)
    cot_lo = arrive(layout_lo, out_grad)
    cot_hi = arrive(layout_hi, out_grad)
    (cot_lo, cot_hi), tok_blocks = lax.optimization_barrier(((cot_lo, cot_hi), tok_blocks))
    forward = [forward_rows(block, weights) for block in tok_blocks]
    fwd_parts = [f[2] for f in forward]
    cot_blocks = group_rows(cot_lo, cot_hi)
    fwd_received = sum_start(fwd_parts)
    fwd_received, cot_blocks = lax.optimization_barrier((fwd_received, cot_blocks))
    fwd_total = sum_finish(fwd_parts, fwd_received)
    grad_parts = [
        backward_rows(block, f[0], f[1], weights) for block, f in zip(cot_blocks, forward)
    ]
    fwd_total, grad_parts = lax.optimization_barrier((fwd_total, grad_parts))

    def home(totals):
        back_lo = return_rows(totals[0], experts, half_slots, model_width)
        back_hi = return_rows(totals[1], experts, half_slots, model_width)
        return collect(layout_lo, back_lo) + collect(layout_hi, back_hi)

    expert_out = home(fwd_total)
    combined = (combine[:, None] * expert_out).astype(jnp.bfloat16)
    combine_grad = jnp.sum(expert_out * cotangent_wide, 1)
    input_grad = home(sum_finish(grad_parts, sum_start(grad_parts)))
    token_grad = input_grad.astype(jnp.bfloat16)
    return (combined, token_grad, combine_grad)


def solution(mesh):
    return jax.shard_map(
        shards,
        mesh=mesh,
        in_specs=(
            P(("dp", "expert"), None),
            P(("dp", "expert"), None),
            P(("dp", "expert")),
            P(("dp", "expert")),
            P("expert", None, "dp", None),
        ),
        out_specs=(P(("dp", "expert"), None), P(("dp", "expert"), None), P(("dp", "expert"))),
        check_vma=False,
    )
```

```python
import jax
import jax.numpy as jnp
from jax import lax
from jax.sharding import PartitionSpec as P


def placement(member, slot_count):
    within = jnp.sum((jnp.cumsum(member, 0) - 1) * member, 1)
    owner_group = jnp.sum(member * lax.iota(jnp.int32, member.shape[1])[None, :], 1)
    is_used = jnp.sum(member, 1) > 0
    target = owner_group * slot_count + within
    buffer_cells = lax.iota(jnp.int32, member.shape[1] * slot_count)
    return ((buffer_cells[:, None] == target[None, :]) & is_used[None, :]).astype(jnp.bfloat16)


def spread(layout, row_block):
    return jnp.dot(layout, row_block, preferred_element_type=jnp.float32).astype(jnp.bfloat16)


def collect(layout, buffer_rows):
    return lax.dot_general(
        layout, buffer_rows, (((0,), (0,)), ((), ())), preferred_element_type=jnp.float32
    )


def shifted(values, step):
    n = lax.axis_size("dp")
    return lax.ppermute(values, "dp", perm=[(i, (i + step) % n) for i in range(n)])


def group_rows(values):
    half = values.shape[0] // 2
    left_lo = shifted(values[:half], 1)
    right_hi = shifted(values[half:], -1)
    far_head = shifted(left_lo, 1)
    far_tail = shifted(right_hi, -1)
    left_hi = shifted(values[half:], 1)
    right_lo = shifted(values[:half], -1)
    return [values, left_lo, left_hi, right_lo, right_hi, far_head, far_tail]


def sum_start(parts):
    far_head = shifted(parts[5].astype(jnp.bfloat16), -1)
    far_tail = shifted(parts[6].astype(jnp.bfloat16), 1)
    return far_head, far_tail


def sum_finish(parts, received):
    own, left_lo, left_hi, right_lo, right_hi = parts[:5]
    far_head, far_tail = [r.astype(jnp.float32) for r in received]

    def wide(x):
        return x.astype(jnp.bfloat16).astype(jnp.float32)

    back_hi_a = shifted(left_hi.astype(jnp.bfloat16), -1).astype(jnp.float32)
    back_lo_b = shifted(right_lo.astype(jnp.bfloat16), 1).astype(jnp.float32)
    back_lo_a = shifted((wide(left_lo) + far_head).astype(jnp.bfloat16), -1).astype(jnp.float32)
    back_hi_b = shifted((wide(right_hi) + far_tail).astype(jnp.bfloat16), 1).astype(jnp.float32)
    return wide(own) + jnp.concatenate([back_lo_a + back_lo_b, back_hi_a + back_hi_b], 0)


def arrive_rows(cold_buf, experts, slot_count, model_width):
    return lax.all_to_all(
        cold_buf.reshape(experts, slot_count, model_width),
        "expert",
        split_axis=0,
        concat_axis=0,
        tiled=True,
    ).reshape(-1, model_width)


def return_rows(total, experts, slot_count, model_width):
    summed = total.astype(jnp.bfloat16).reshape(experts, slot_count, model_width)
    return lax.all_to_all(summed, "expert", split_axis=0, concat_axis=0, tiled=True).reshape(
        -1, model_width
    )


def forward_rows(row_block, matrices):
    gate_up = jnp.einsum("rd,kfd->krf", row_block, matrices[:2], preferred_element_type=jnp.float32)
    gate_act = gate_up[0]
    up_act = gate_up[1]
    hidden = (gate_act * jax.nn.sigmoid(gate_act) * up_act).astype(jnp.bfloat16)
    partial_out = jnp.dot(hidden, matrices[2], preferred_element_type=jnp.float32)
    return (gate_act, up_act, partial_out)


def backward_rows(row_block, gate_act, up_act, matrices):
    hidden_grad = lax.dot_general(
        row_block, matrices[2], (((1,), (1,)), ((), ())), preferred_element_type=jnp.float32
    )
    squashed = jax.nn.sigmoid(gate_act)
    gate_grad = (hidden_grad * up_act * squashed * (1.0 + gate_act * (1.0 - squashed))).astype(
        jnp.bfloat16
    )
    up_grad = (hidden_grad * gate_act * squashed).astype(jnp.bfloat16)
    both_grads = jnp.stack([gate_grad, up_grad])
    return jnp.einsum("krf,kfd->rd", both_grads, matrices[:2], preferred_element_type=jnp.float32)


def shards(tokens, cotangent, routes, combine, expert_weights):
    weights = expert_weights[0]
    tok_dev = tokens.shape[0]
    model_width = tokens.shape[1]
    experts = lax.axis_size("expert")
    capacity = 2 * tok_dev // experts
    labels = lax.iota(jnp.int32, experts)
    member = (routes[:, None] == labels[None, :]).astype(jnp.int32)
    cold_layout = placement(member, capacity)
    cold_buf = spread(cold_layout, tokens)
    tok_blocks = group_rows(arrive_rows(cold_buf, experts, capacity, model_width))
    cotangent_wide = cotangent.astype(jnp.float32)
    out_grad = (combine[:, None] * cotangent_wide).astype(jnp.bfloat16)
    cold_grad_buf = spread(cold_layout, out_grad)
    cold_grad_arrived = arrive_rows(cold_grad_buf, experts, capacity, model_width)
    cold_grad_arrived, tok_blocks = lax.optimization_barrier((cold_grad_arrived, tok_blocks))
    cot_blocks = group_rows(cold_grad_arrived)
    tok_blocks, cot_blocks[1] = lax.optimization_barrier((tok_blocks, cot_blocks[1]))
    forward = [forward_rows(block, weights) for block in tok_blocks]
    fwd_parts = [f[2] for f in forward]
    fwd_received = sum_start(fwd_parts)
    fwd_received, cot_blocks = lax.optimization_barrier((fwd_received, cot_blocks))
    fwd_total = sum_finish(fwd_parts, fwd_received)
    grad_parts = [
        backward_rows(block, f[0], f[1], weights) for block, f in zip(cot_blocks, forward)
    ]
    fwd_total, grad_parts = lax.optimization_barrier((fwd_total, grad_parts))
    cold_out = return_rows(fwd_total, experts, capacity, model_width)
    expert_out = collect(cold_layout, cold_out)
    combined = (combine[:, None] * expert_out).astype(jnp.bfloat16)
    combine_grad = jnp.sum(expert_out * cotangent_wide, 1)
    grad_total = sum_finish(grad_parts, sum_start(grad_parts))
    cold_grad_out = return_rows(grad_total, experts, capacity, model_width)
    input_grad = collect(cold_layout, cold_grad_out)
    token_grad = input_grad.astype(jnp.bfloat16)
    return (combined, token_grad, combine_grad)


def solution(mesh):
    return jax.shard_map(
        shards,
        mesh=mesh,
        in_specs=(
            P(("dp", "expert"), None),
            P(("dp", "expert"), None),
            P(("dp", "expert")),
            P(("dp", "expert")),
            P("expert", None, "dp", None),
        ),
        out_specs=(P(("dp", "expert"), None), P(("dp", "expert"), None), P(("dp", "expert"))),
        check_vma=False,
    )
```

```python
import jax
import jax.numpy as jnp
from jax import lax
from jax.sharding import PartitionSpec as P


def placement(member, slot_count):
    within = jnp.sum((jnp.cumsum(member, 0) - 1) * member, 1)
    owner_group = jnp.sum(member * lax.iota(jnp.int32, member.shape[1])[None, :], 1)
    is_used = jnp.sum(member, 1) > 0
    target = owner_group * slot_count + within
    buffer_cells = lax.iota(jnp.int32, member.shape[1] * slot_count)
    return ((buffer_cells[:, None] == target[None, :]) & is_used[None, :]).astype(jnp.bfloat16)


def spread(layout, row_block):
    return jnp.dot(layout, row_block, preferred_element_type=jnp.float32).astype(jnp.bfloat16)


def collect(layout, buffer_rows):
    return lax.dot_general(
        layout, buffer_rows, (((0,), (0,)), ((), ())), preferred_element_type=jnp.float32
    )


def shifted(values, step):
    n = lax.axis_size("dp")
    return lax.ppermute(values, "dp", perm=[(i, (i + step) % n) for i in range(n)])


def group_rows(values):
    half = values.shape[0] // 2
    left_lo = shifted(values[:half], 1)
    right_hi = shifted(values[half:], -1)
    far_head = shifted(left_lo, 1)
    far_tail = shifted(right_hi, -1)
    left_hi = shifted(values[half:], 1)
    right_lo = shifted(values[:half], -1)
    return [values, left_lo, left_hi, right_lo, right_hi, far_head, far_tail]


def sum_start(parts):
    far_head = shifted(parts[5].astype(jnp.bfloat16), -1)
    far_tail = shifted(parts[6].astype(jnp.bfloat16), 1)
    return far_head, far_tail


def sum_finish(parts, received):
    own, left_lo, left_hi, right_lo, right_hi = parts[:5]
    far_head, far_tail = [r.astype(jnp.float32) for r in received]

    def wide(x):
        return x.astype(jnp.bfloat16).astype(jnp.float32)

    back_hi_a = shifted(left_hi.astype(jnp.bfloat16), -1).astype(jnp.float32)
    back_lo_b = shifted(right_lo.astype(jnp.bfloat16), 1).astype(jnp.float32)
    back_lo_a = shifted((wide(left_lo) + far_head).astype(jnp.bfloat16), -1).astype(jnp.float32)
    back_hi_b = shifted((wide(right_hi) + far_tail).astype(jnp.bfloat16), 1).astype(jnp.float32)
    return wide(own) + jnp.concatenate([back_lo_a + back_lo_b, back_hi_a + back_hi_b], 0)


def arrive_rows(cold_buf, experts, slot_count, model_width):
    return lax.all_to_all(
        cold_buf.reshape(experts, slot_count, model_width),
        "expert",
        split_axis=0,
        concat_axis=0,
        tiled=True,
    ).reshape(-1, model_width)


def return_rows(total, experts, slot_count, model_width):
    summed = total.astype(jnp.bfloat16).reshape(experts, slot_count, model_width)
    return lax.all_to_all(summed, "expert", split_axis=0, concat_axis=0, tiled=True).reshape(
        -1, model_width
    )


def forward_rows(row_block, matrices):
    gate_up = jnp.einsum("rd,kfd->krf", row_block, matrices[:2], preferred_element_type=jnp.float32)
    gate_act = gate_up[0]
    up_act = gate_up[1]
    hidden = (gate_act * jax.nn.sigmoid(gate_act) * up_act).astype(jnp.bfloat16)
    partial_out = jnp.dot(hidden, matrices[2], preferred_element_type=jnp.float32)
    return (gate_act, up_act, partial_out)


def backward_rows(row_block, gate_act, up_act, matrices):
    hidden_grad = lax.dot_general(
        row_block, matrices[2], (((1,), (1,)), ((), ())), preferred_element_type=jnp.float32
    )
    squashed = jax.nn.sigmoid(gate_act)
    gate_grad = (hidden_grad * up_act * squashed * (1.0 + gate_act * (1.0 - squashed))).astype(
        jnp.bfloat16
    )
    up_grad = (hidden_grad * gate_act * squashed).astype(jnp.bfloat16)
    both_grads = jnp.stack([gate_grad, up_grad])
    return jnp.einsum("krf,kfd->rd", both_grads, matrices[:2], preferred_element_type=jnp.float32)


def joined(blocks):
    return [blocks[0], jnp.concatenate(blocks[1:], 0)]


def halves(parts):
    rest = parts[1]
    size = rest.shape[0] // 6
    return [parts[0]] + [rest[k * size:(k + 1) * size] for k in range(6)]


def shards(tokens, cotangent, routes, combine, expert_weights):
    weights = expert_weights[0]
    tok_dev = tokens.shape[0]
    model_width = tokens.shape[1]
    experts = lax.axis_size("expert")
    capacity = 2 * tok_dev // experts
    labels = lax.iota(jnp.int32, experts)
    member = (routes[:, None] == labels[None, :]).astype(jnp.int32)
    cold_layout = placement(member, capacity)
    cold_buf = spread(cold_layout, tokens)
    tok_blocks = group_rows(arrive_rows(cold_buf, experts, capacity, model_width))
    cotangent_wide = cotangent.astype(jnp.float32)
    out_grad = (combine[:, None] * cotangent_wide).astype(jnp.bfloat16)
    cold_grad_buf = spread(cold_layout, out_grad)
    cold_grad_arrived = arrive_rows(cold_grad_buf, experts, capacity, model_width)
    cold_grad_arrived, tok_blocks = lax.optimization_barrier((cold_grad_arrived, tok_blocks))
    forward = [forward_rows(block, weights) for block in joined(tok_blocks)]
    fwd_parts = halves([f[2] for f in forward])
    cot_blocks = group_rows(cold_grad_arrived)
    fwd_received = sum_start(fwd_parts)
    fwd_received, cot_blocks = lax.optimization_barrier((fwd_received, cot_blocks))
    fwd_total = sum_finish(fwd_parts, fwd_received)
    grad_parts = halves(
        [backward_rows(block, f[0], f[1], weights) for block, f in zip(joined(cot_blocks), forward)]
    )
    fwd_total, grad_parts = lax.optimization_barrier((fwd_total, grad_parts))
    cold_out = return_rows(fwd_total, experts, capacity, model_width)
    expert_out = collect(cold_layout, cold_out)
    combined = (combine[:, None] * expert_out).astype(jnp.bfloat16)
    combine_grad = jnp.sum(expert_out * cotangent_wide, 1)
    grad_total = sum_finish(grad_parts, sum_start(grad_parts))
    cold_grad_out = return_rows(grad_total, experts, capacity, model_width)
    input_grad = collect(cold_layout, cold_grad_out)
    token_grad = input_grad.astype(jnp.bfloat16)
    return (combined, token_grad, combine_grad)


def solution(mesh):
    return jax.shard_map(
        shards,
        mesh=mesh,
        in_specs=(
            P(("dp", "expert"), None),
            P(("dp", "expert"), None),
            P(("dp", "expert")),
            P(("dp", "expert")),
            P("expert", None, "dp", None),
        ),
        out_specs=(P(("dp", "expert"), None), P(("dp", "expert"), None), P(("dp", "expert"))),
        check_vma=False,
    )
```

```python
import jax
import jax.numpy as jnp
from jax import lax
from jax.sharding import PartitionSpec as P


def placement(member, slot_count):
    within = jnp.sum((jnp.cumsum(member, 0) - 1) * member, 1)
    owner_group = jnp.sum(member * lax.iota(jnp.int32, member.shape[1])[None, :], 1)
    is_used = jnp.sum(member, 1) > 0
    target = owner_group * slot_count + within
    buffer_cells = lax.iota(jnp.int32, member.shape[1] * slot_count)
    return ((buffer_cells[:, None] == target[None, :]) & is_used[None, :]).astype(jnp.bfloat16)


def spread(layout, row_block):
    return jnp.dot(layout, row_block, preferred_element_type=jnp.float32).astype(jnp.bfloat16)


def collect(layout, buffer_rows):
    return lax.dot_general(
        layout, buffer_rows, (((0,), (0,)), ((), ())), preferred_element_type=jnp.float32
    )


def shifted(values, step):
    n = lax.axis_size("dp")
    return lax.ppermute(values, "dp", perm=[(i, (i + step) % n) for i in range(n)])


def group_rows(values):
    half = values.shape[0] // 2
    left_lo = shifted(values[:half], 1)
    right_hi = shifted(values[half:], -1)
    far_head = shifted(left_lo, 1)
    far_tail = shifted(right_hi, -1)
    left_hi = shifted(values[half:], 1)
    right_lo = shifted(values[:half], -1)
    return [values, left_lo, left_hi, right_lo, right_hi, far_head, far_tail]


def sum_start(parts):
    far_head = shifted(parts[5].astype(jnp.bfloat16), -1)
    far_tail = shifted(parts[6].astype(jnp.bfloat16), 1)
    return far_head, far_tail


def sum_finish(parts, received):
    own, left_lo, left_hi, right_lo, right_hi = parts[:5]
    far_head, far_tail = [r.astype(jnp.float32) for r in received]

    def wide(x):
        return x.astype(jnp.bfloat16).astype(jnp.float32)

    back_hi_a = shifted(left_hi.astype(jnp.bfloat16), -1).astype(jnp.float32)
    back_lo_b = shifted(right_lo.astype(jnp.bfloat16), 1).astype(jnp.float32)
    back_lo_a = shifted((wide(left_lo) + far_head).astype(jnp.bfloat16), -1).astype(jnp.float32)
    back_hi_b = shifted((wide(right_hi) + far_tail).astype(jnp.bfloat16), 1).astype(jnp.float32)
    return wide(own) + jnp.concatenate([back_lo_a + back_lo_b, back_hi_a + back_hi_b], 0)


def arrive_rows(cold_buf, experts, slot_count, model_width):
    return lax.all_to_all(
        cold_buf.reshape(experts, slot_count, model_width),
        "expert",
        split_axis=0,
        concat_axis=0,
        tiled=True,
    ).reshape(-1, model_width)


def return_rows(total, experts, slot_count, model_width):
    summed = total.astype(jnp.bfloat16).reshape(experts, slot_count, model_width)
    return lax.all_to_all(summed, "expert", split_axis=0, concat_axis=0, tiled=True).reshape(
        -1, model_width
    )


def forward_rows(row_block, matrices):
    gate_up = jnp.einsum("rd,kfd->krf", row_block, matrices[:2], preferred_element_type=jnp.float32)
    gate_act = gate_up[0]
    up_act = gate_up[1]
    hidden = (gate_act * jax.nn.sigmoid(gate_act) * up_act).astype(jnp.bfloat16)
    partial_out = jnp.dot(hidden, matrices[2], preferred_element_type=jnp.float32)
    return (gate_act, up_act, partial_out)


def backward_rows(row_block, gate_act, up_act, matrices):
    hidden_grad = lax.dot_general(
        row_block, matrices[2], (((1,), (1,)), ((), ())), preferred_element_type=jnp.float32
    )
    squashed = jax.nn.sigmoid(gate_act)
    gate_grad = (hidden_grad * up_act * squashed * (1.0 + gate_act * (1.0 - squashed))).astype(
        jnp.bfloat16
    )
    up_grad = (hidden_grad * gate_act * squashed).astype(jnp.bfloat16)
    both_grads = jnp.stack([gate_grad, up_grad])
    return jnp.einsum("krf,kfd->rd", both_grads, matrices[:2], preferred_element_type=jnp.float32)


def joined(blocks):
    return [blocks[0]] + [jnp.concatenate(blocks[k:k + 2], 0) for k in (1, 3, 5)]


def halves(parts):
    out = [parts[0]]
    for part in parts[1:]:
        half = part.shape[0] // 2
        out += [part[:half], part[half:]]
    return out


def shards(tokens, cotangent, routes, combine, expert_weights):
    weights = expert_weights[0]
    tok_dev = tokens.shape[0]
    model_width = tokens.shape[1]
    experts = lax.axis_size("expert")
    capacity = 2 * tok_dev // experts
    labels = lax.iota(jnp.int32, experts)
    member = (routes[:, None] == labels[None, :]).astype(jnp.int32)
    cold_layout = placement(member, capacity)
    cold_buf = spread(cold_layout, tokens)
    tok_blocks = group_rows(arrive_rows(cold_buf, experts, capacity, model_width))
    cotangent_wide = cotangent.astype(jnp.float32)
    out_grad = (combine[:, None] * cotangent_wide).astype(jnp.bfloat16)
    cold_grad_buf = spread(cold_layout, out_grad)
    cold_grad_arrived = arrive_rows(cold_grad_buf, experts, capacity, model_width)
    cold_grad_arrived, tok_blocks = lax.optimization_barrier((cold_grad_arrived, tok_blocks))
    forward = [forward_rows(block, weights) for block in joined(tok_blocks)]
    fwd_parts = halves([f[2] for f in forward])
    cot_blocks = group_rows(cold_grad_arrived)
    fwd_received = sum_start(fwd_parts)
    fwd_received, cot_blocks = lax.optimization_barrier((fwd_received, cot_blocks))
    fwd_total = sum_finish(fwd_parts, fwd_received)
    grad_parts = halves(
        [backward_rows(block, f[0], f[1], weights) for block, f in zip(joined(cot_blocks), forward)]
    )
    fwd_total, grad_parts = lax.optimization_barrier((fwd_total, grad_parts))
    cold_out = return_rows(fwd_total, experts, capacity, model_width)
    expert_out = collect(cold_layout, cold_out)
    combined = (combine[:, None] * expert_out).astype(jnp.bfloat16)
    combine_grad = jnp.sum(expert_out * cotangent_wide, 1)
    grad_total = sum_finish(grad_parts, sum_start(grad_parts))
    cold_grad_out = return_rows(grad_total, experts, capacity, model_width)
    input_grad = collect(cold_layout, cold_grad_out)
    token_grad = input_grad.astype(jnp.bfloat16)
    return (combined, token_grad, combine_grad)


def solution(mesh):
    return jax.shard_map(
        shards,
        mesh=mesh,
        in_specs=(
            P(("dp", "expert"), None),
            P(("dp", "expert"), None),
            P(("dp", "expert")),
            P(("dp", "expert")),
            P("expert", None, "dp", None),
        ),
        out_specs=(P(("dp", "expert"), None), P(("dp", "expert"), None), P(("dp", "expert"))),
        check_vma=False,
    )
```

```python
import jax
import jax.numpy as jnp
from jax import lax
from jax.sharding import PartitionSpec as P


def placement(member, slot_count):
    within = jnp.sum((jnp.cumsum(member, 0) - 1) * member, 1)
    owner_group = jnp.sum(member * lax.iota(jnp.int32, member.shape[1])[None, :], 1)
    is_used = jnp.sum(member, 1) > 0
    target = owner_group * slot_count + within
    buffer_cells = lax.iota(jnp.int32, member.shape[1] * slot_count)
    return ((buffer_cells[:, None] == target[None, :]) & is_used[None, :]).astype(jnp.bfloat16)


def spread(layout, row_block):
    return jnp.dot(layout, row_block, preferred_element_type=jnp.float32).astype(jnp.bfloat16)


def collect(layout, buffer_rows):
    return lax.dot_general(
        layout, buffer_rows, (((0,), (0,)), ((), ())), preferred_element_type=jnp.float32
    )


def shifted(values, step):
    n = lax.axis_size("dp")
    return lax.ppermute(values, "dp", perm=[(i, (i + step) % n) for i in range(n)])


def group_rows(values):
    half = values.shape[0] // 2
    left_lo = shifted(values[:half], 1)
    right_hi = shifted(values[half:], -1)
    far_head = shifted(left_lo, 1)
    far_tail = shifted(right_hi, -1)
    left_hi = shifted(values[half:], 1)
    right_lo = shifted(values[:half], -1)
    return [values, left_lo, left_hi, right_lo, right_hi, far_head, far_tail]


def sum_start(parts):
    far_head = shifted(parts[5].astype(jnp.bfloat16), -1)
    far_tail = shifted(parts[6].astype(jnp.bfloat16), 1)
    return far_head, far_tail


def sum_finish(parts, received):
    own, left_lo, left_hi, right_lo, right_hi = parts[:5]
    far_head, far_tail = [r.astype(jnp.float32) for r in received]

    def wide(x):
        return x.astype(jnp.bfloat16).astype(jnp.float32)

    back_hi_a = shifted(left_hi.astype(jnp.bfloat16), -1).astype(jnp.float32)
    back_lo_b = shifted(right_lo.astype(jnp.bfloat16), 1).astype(jnp.float32)
    back_lo_a = shifted((wide(left_lo) + far_head).astype(jnp.bfloat16), -1).astype(jnp.float32)
    back_hi_b = shifted((wide(right_hi) + far_tail).astype(jnp.bfloat16), 1).astype(jnp.float32)
    return wide(own) + jnp.concatenate([back_lo_a + back_lo_b, back_hi_a + back_hi_b], 0)


def arrive_rows(cold_buf, experts, slot_count, model_width):
    return lax.all_to_all(
        cold_buf.reshape(experts, slot_count, model_width),
        "expert",
        split_axis=0,
        concat_axis=0,
        tiled=True,
    ).reshape(-1, model_width)


def return_rows(total, experts, slot_count, model_width):
    summed = total.astype(jnp.bfloat16).reshape(experts, slot_count, model_width)
    return lax.all_to_all(summed, "expert", split_axis=0, concat_axis=0, tiled=True).reshape(
        -1, model_width
    )


def forward_rows(row_block, matrices):
    gate_up = jnp.einsum("rd,kfd->krf", row_block, matrices[:2], preferred_element_type=jnp.float32)
    gate_act = gate_up[0]
    up_act = gate_up[1]
    hidden = (gate_act * jax.nn.sigmoid(gate_act) * up_act).astype(jnp.bfloat16)
    partial_out = jnp.dot(hidden, matrices[2], preferred_element_type=jnp.float32)
    return (gate_act, up_act, partial_out)


def backward_rows(row_block, gate_act, up_act, matrices):
    hidden_grad = lax.dot_general(
        row_block, matrices[2], (((1,), (1,)), ((), ())), preferred_element_type=jnp.float32
    )
    squashed = jax.nn.sigmoid(gate_act)
    gate_grad = (hidden_grad * up_act * squashed * (1.0 + gate_act * (1.0 - squashed))).astype(
        jnp.bfloat16
    )
    up_grad = (hidden_grad * gate_act * squashed).astype(jnp.bfloat16)
    both_grads = jnp.stack([gate_grad, up_grad])
    return jnp.einsum("krf,kfd->rd", both_grads, matrices[:2], preferred_element_type=jnp.float32)


def shards(tokens, cotangent, routes, combine, expert_weights):
    weights = expert_weights[0]
    tok_dev = tokens.shape[0]
    model_width = tokens.shape[1]
    experts = lax.axis_size("expert")
    capacity = 2 * tok_dev // experts
    labels = lax.iota(jnp.int32, experts)
    member = (routes[:, None] == labels[None, :]).astype(jnp.int32)
    cold_layout = placement(member, capacity)
    cold_buf = spread(cold_layout, tokens)
    tok_blocks = group_rows(arrive_rows(cold_buf, experts, capacity, model_width))
    cotangent_wide = cotangent.astype(jnp.float32)
    out_grad = (combine[:, None] * cotangent_wide).astype(jnp.bfloat16)
    cold_grad_buf = spread(cold_layout, out_grad)
    cold_grad_arrived = arrive_rows(cold_grad_buf, experts, capacity, model_width)
    cold_grad_arrived, tok_blocks = lax.optimization_barrier((cold_grad_arrived, tok_blocks))
    forward = [forward_rows(block, weights) for block in tok_blocks]
    fwd_parts = [f[2] for f in forward]
    cot_blocks = group_rows(cold_grad_arrived)
    fwd_received = sum_start(fwd_parts)
    fwd_received, cot_blocks = lax.optimization_barrier((fwd_received, cot_blocks))
    fwd_total = sum_finish(fwd_parts, fwd_received)
    grad_parts = [
        backward_rows(block, f[0], f[1], weights) for block, f in zip(cot_blocks, forward)
    ]
    grad_received = sum_start(grad_parts)
    fwd_total, grad_received = lax.optimization_barrier((fwd_total, grad_received))
    cold_out = return_rows(fwd_total, experts, capacity, model_width)
    expert_out = collect(cold_layout, cold_out)
    combined = (combine[:, None] * expert_out).astype(jnp.bfloat16)
    combine_grad = jnp.sum(expert_out * cotangent_wide, 1)
    grad_total = sum_finish(grad_parts, grad_received)
    cold_grad_out = return_rows(grad_total, experts, capacity, model_width)
    input_grad = collect(cold_layout, cold_grad_out)
    token_grad = input_grad.astype(jnp.bfloat16)
    return (combined, token_grad, combine_grad)


def solution(mesh):
    return jax.shard_map(
        shards,
        mesh=mesh,
        in_specs=(
            P(("dp", "expert"), None),
            P(("dp", "expert"), None),
            P(("dp", "expert")),
            P(("dp", "expert")),
            P("expert", None, "dp", None),
        ),
        out_specs=(P(("dp", "expert"), None), P(("dp", "expert"), None), P(("dp", "expert"))),
        check_vma=False,
    )
```

```python
import jax
import jax.numpy as jnp
from jax import lax
from jax.sharding import PartitionSpec as P


def placement(member, slot_count):
    within = jnp.sum((jnp.cumsum(member, 0) - 1) * member, 1)
    owner_group = jnp.sum(member * lax.iota(jnp.int32, member.shape[1])[None, :], 1)
    is_used = jnp.sum(member, 1) > 0
    target = owner_group * slot_count + within
    buffer_cells = lax.iota(jnp.int32, member.shape[1] * slot_count)
    return ((buffer_cells[:, None] == target[None, :]) & is_used[None, :]).astype(jnp.bfloat16)


def spread(layout, row_block):
    return jnp.dot(layout, row_block, preferred_element_type=jnp.float32).astype(jnp.bfloat16)


def collect(layout, buffer_rows):
    return lax.dot_general(
        layout, buffer_rows, (((0,), (0,)), ((), ())), preferred_element_type=jnp.float32
    )


def shifted(values, step):
    n = lax.axis_size("dp")
    return lax.ppermute(values, "dp", perm=[(i, (i + step) % n) for i in range(n)])


def group_rows(values):
    half = values.shape[0] // 2
    left_lo = shifted(values[:half], 1)
    right_hi = shifted(values[half:], -1)
    far_head = shifted(left_lo, 1)
    far_tail = shifted(right_hi, -1)
    left_hi = shifted(values[half:], 1)
    right_lo = shifted(values[:half], -1)
    return [values, left_lo, left_hi, right_lo, right_hi, far_head, far_tail]


def sum_start(parts):
    far_head = shifted(parts[5].astype(jnp.bfloat16), -1)
    far_tail = shifted(parts[6].astype(jnp.bfloat16), 1)
    return far_head, far_tail


def sum_finish(parts, received):
    own, left_lo, left_hi, right_lo, right_hi = parts[:5]
    far_head, far_tail = [r.astype(jnp.float32) for r in received]

    def wide(x):
        return x.astype(jnp.bfloat16).astype(jnp.float32)

    back_hi_a = shifted(left_hi.astype(jnp.bfloat16), -1).astype(jnp.float32)
    back_lo_b = shifted(right_lo.astype(jnp.bfloat16), 1).astype(jnp.float32)
    back_lo_a = shifted((wide(left_lo) + far_head).astype(jnp.bfloat16), -1).astype(jnp.float32)
    back_hi_b = shifted((wide(right_hi) + far_tail).astype(jnp.bfloat16), 1).astype(jnp.float32)
    return wide(own) + jnp.concatenate([back_lo_a + back_lo_b, back_hi_a + back_hi_b], 0)


def arrive_rows(cold_buf, experts, slot_count, model_width):
    return lax.all_to_all(
        cold_buf.reshape(experts, slot_count, model_width),
        "expert",
        split_axis=0,
        concat_axis=0,
        tiled=True,
    ).reshape(-1, model_width)


def return_rows(total, experts, slot_count, model_width):
    summed = total.astype(jnp.bfloat16).reshape(experts, slot_count, model_width)
    return lax.all_to_all(summed, "expert", split_axis=0, concat_axis=0, tiled=True).reshape(
        -1, model_width
    )


def forward_rows(row_block, matrices):
    gate_up = jnp.einsum("rd,kfd->krf", row_block, matrices[:2], preferred_element_type=jnp.float32)
    gate_act = gate_up[0]
    up_act = gate_up[1]
    hidden = (gate_act * jax.nn.sigmoid(gate_act) * up_act).astype(jnp.bfloat16)
    partial_out = jnp.dot(hidden, matrices[2], preferred_element_type=jnp.float32)
    return (gate_act, up_act, partial_out)


def backward_rows(row_block, gate_act, up_act, matrices):
    hidden_grad = lax.dot_general(
        row_block, matrices[2], (((1,), (1,)), ((), ())), preferred_element_type=jnp.float32
    )
    squashed = jax.nn.sigmoid(gate_act)
    gate_grad = (hidden_grad * up_act * squashed * (1.0 + gate_act * (1.0 - squashed))).astype(
        jnp.bfloat16
    )
    up_grad = (hidden_grad * gate_act * squashed).astype(jnp.bfloat16)
    both_grads = jnp.stack([gate_grad, up_grad])
    return jnp.einsum("krf,kfd->rd", both_grads, matrices[:2], preferred_element_type=jnp.float32)


def shards(tokens, cotangent, routes, combine, expert_weights):
    weights = expert_weights[0]
    tok_dev = tokens.shape[0]
    model_width = tokens.shape[1]
    experts = lax.axis_size("expert")
    capacity = 2 * tok_dev // experts
    labels = lax.iota(jnp.int32, experts)
    member = (routes[:, None] == labels[None, :]).astype(jnp.int32)
    cold_layout = placement(member, capacity)
    cold_buf = spread(cold_layout, tokens)
    tok_blocks = group_rows(arrive_rows(cold_buf, experts, capacity, model_width))
    cotangent_wide = cotangent.astype(jnp.float32)
    out_grad = (combine[:, None] * cotangent_wide).astype(jnp.bfloat16)
    cold_grad_buf = spread(cold_layout, out_grad)
    cold_grad_arrived = arrive_rows(cold_grad_buf, experts, capacity, model_width)
    cold_grad_arrived, tok_blocks = lax.optimization_barrier((cold_grad_arrived, tok_blocks))
    forward = [forward_rows(block, weights) for block in tok_blocks]
    fwd_parts = [f[2] for f in forward]
    cot_blocks = group_rows(cold_grad_arrived)
    fwd_received = sum_start(fwd_parts)
    fwd_received, cot_blocks[5:] = lax.optimization_barrier((fwd_received, cot_blocks[5:]))
    fwd_total = sum_finish(fwd_parts, fwd_received)
    grad_parts = [
        backward_rows(block, f[0], f[1], weights) for block, f in zip(cot_blocks, forward)
    ]
    grad_received = sum_start(grad_parts)
    fwd_total, grad_received = lax.optimization_barrier((fwd_total, grad_received))
    cold_out = return_rows(fwd_total, experts, capacity, model_width)
    expert_out = collect(cold_layout, cold_out)
    combined = (combine[:, None] * expert_out).astype(jnp.bfloat16)
    combine_grad = jnp.sum(expert_out * cotangent_wide, 1)
    grad_total = sum_finish(grad_parts, grad_received)
    cold_grad_out = return_rows(grad_total, experts, capacity, model_width)
    input_grad = collect(cold_layout, cold_grad_out)
    token_grad = input_grad.astype(jnp.bfloat16)
    return (combined, token_grad, combine_grad)


def solution(mesh):
    return jax.shard_map(
        shards,
        mesh=mesh,
        in_specs=(
            P(("dp", "expert"), None),
            P(("dp", "expert"), None),
            P(("dp", "expert")),
            P(("dp", "expert")),
            P("expert", None, "dp", None),
        ),
        out_specs=(P(("dp", "expert"), None), P(("dp", "expert"), None), P(("dp", "expert"))),
        check_vma=False,
    )
```

```python
import jax
import jax.numpy as jnp
from jax import lax
from jax.sharding import PartitionSpec as P


def placement(member, slot_count):
    within = jnp.sum((jnp.cumsum(member, 0) - 1) * member, 1)
    owner_group = jnp.sum(member * lax.iota(jnp.int32, member.shape[1])[None, :], 1)
    is_used = jnp.sum(member, 1) > 0
    target = owner_group * slot_count + within
    buffer_cells = lax.iota(jnp.int32, member.shape[1] * slot_count)
    return ((buffer_cells[:, None] == target[None, :]) & is_used[None, :]).astype(jnp.bfloat16)


def spread(layout, row_block):
    return jnp.dot(layout, row_block, preferred_element_type=jnp.float32).astype(jnp.bfloat16)


def collect(layout, buffer_rows):
    return lax.dot_general(
        layout, buffer_rows, (((0,), (0,)), ((), ())), preferred_element_type=jnp.float32
    )


def shifted(values, step):
    n = lax.axis_size("dp")
    return lax.ppermute(values, "dp", perm=[(i, (i + step) % n) for i in range(n)])


def group_rows(values):
    half = values.shape[0] // 2
    left_lo = shifted(values[:half], 1)
    right_hi = shifted(values[half:], -1)
    far_head = shifted(left_lo, 1)
    far_tail = shifted(right_hi, -1)
    left_hi = shifted(values[half:], 1)
    right_lo = shifted(values[:half], -1)
    return [values, left_lo, left_hi, right_lo, right_hi, far_head, far_tail]


def sum_start(parts):
    far_head = shifted(parts[5].astype(jnp.bfloat16), -1)
    far_tail = shifted(parts[6].astype(jnp.bfloat16), 1)
    return far_head, far_tail


def sum_finish(parts, received):
    own, left_lo, left_hi, right_lo, right_hi = parts[:5]
    far_head, far_tail = [r.astype(jnp.float32) for r in received]

    def wide(x):
        return x.astype(jnp.bfloat16).astype(jnp.float32)

    back_hi_a = shifted(left_hi.astype(jnp.bfloat16), -1).astype(jnp.float32)
    back_lo_b = shifted(right_lo.astype(jnp.bfloat16), 1).astype(jnp.float32)
    back_lo_a = shifted((wide(left_lo) + far_head).astype(jnp.bfloat16), -1).astype(jnp.float32)
    back_hi_b = shifted((wide(right_hi) + far_tail).astype(jnp.bfloat16), 1).astype(jnp.float32)
    return wide(own) + jnp.concatenate([back_lo_a + back_lo_b, back_hi_a + back_hi_b], 0)


def arrive_rows(cold_buf, experts, slot_count, model_width):
    return lax.all_to_all(
        cold_buf.reshape(experts, slot_count, model_width),
        "expert",
        split_axis=0,
        concat_axis=0,
        tiled=True,
    ).reshape(-1, model_width)


def return_rows(total, experts, slot_count, model_width):
    summed = total.astype(jnp.bfloat16).reshape(experts, slot_count, model_width)
    return lax.all_to_all(summed, "expert", split_axis=0, concat_axis=0, tiled=True).reshape(
        -1, model_width
    )


def forward_rows(row_block, matrices):
    gate_up = jnp.einsum("rd,kfd->krf", row_block, matrices[:2], preferred_element_type=jnp.float32)
    gate_act = gate_up[0]
    up_act = gate_up[1]
    hidden = (gate_act * jax.nn.sigmoid(gate_act) * up_act).astype(jnp.bfloat16)
    partial_out = jnp.dot(hidden, matrices[2], preferred_element_type=jnp.float32)
    return (gate_act, up_act, partial_out)


def backward_rows(row_block, gate_act, up_act, matrices):
    hidden_grad = lax.dot_general(
        row_block, matrices[2], (((1,), (1,)), ((), ())), preferred_element_type=jnp.float32
    )
    squashed = jax.nn.sigmoid(gate_act)
    gate_grad = (hidden_grad * up_act * squashed * (1.0 + gate_act * (1.0 - squashed))).astype(
        jnp.bfloat16
    )
    up_grad = (hidden_grad * gate_act * squashed).astype(jnp.bfloat16)
    both_grads = jnp.stack([gate_grad, up_grad])
    return jnp.einsum("krf,kfd->rd", both_grads, matrices[:2], preferred_element_type=jnp.float32)


def shards(tokens, cotangent, routes, combine, expert_weights):
    weights = expert_weights[0]
    tok_dev = tokens.shape[0]
    model_width = tokens.shape[1]
    experts = lax.axis_size("expert")
    capacity = 2 * tok_dev // experts
    labels = lax.iota(jnp.int32, experts)
    member = (routes[:, None] == labels[None, :]).astype(jnp.int32)
    cold_layout = placement(member, capacity)
    cold_buf = spread(cold_layout, tokens)
    tok_blocks = group_rows(arrive_rows(cold_buf, experts, capacity, model_width))
    cotangent_wide = cotangent.astype(jnp.float32)
    out_grad = (combine[:, None] * cotangent_wide).astype(jnp.bfloat16)
    cold_grad_buf = spread(cold_layout, out_grad)
    cold_grad_arrived = arrive_rows(cold_grad_buf, experts, capacity, model_width)
    cold_grad_arrived, tok_blocks = lax.optimization_barrier((cold_grad_arrived, tok_blocks))
    forward = [forward_rows(block, weights) for block in tok_blocks]
    fwd_parts = [f[2] for f in forward]
    cot_blocks = group_rows(cold_grad_arrived)
    fwd_received = sum_start(fwd_parts)
    fwd_received, cot_blocks = lax.optimization_barrier((fwd_received, cot_blocks))
    fwd_total = sum_finish(fwd_parts, fwd_received)
    grad_parts = [
        backward_rows(block, f[0], f[1], weights) for block, f in zip(cot_blocks, forward)
    ]
    grad_received = sum_start(grad_parts)
    fwd_total, grad_received, grad_parts[2:4] = lax.optimization_barrier(
        (fwd_total, grad_received, grad_parts[2:4])
    )
    cold_out = return_rows(fwd_total, experts, capacity, model_width)
    expert_out = collect(cold_layout, cold_out)
    combined = (combine[:, None] * expert_out).astype(jnp.bfloat16)
    combine_grad = jnp.sum(expert_out * cotangent_wide, 1)
    grad_total = sum_finish(grad_parts, grad_received)
    cold_grad_out = return_rows(grad_total, experts, capacity, model_width)
    input_grad = collect(cold_layout, cold_grad_out)
    token_grad = input_grad.astype(jnp.bfloat16)
    return (combined, token_grad, combine_grad)


def solution(mesh):
    return jax.shard_map(
        shards,
        mesh=mesh,
        in_specs=(
            P(("dp", "expert"), None),
            P(("dp", "expert"), None),
            P(("dp", "expert")),
            P(("dp", "expert")),
            P("expert", None, "dp", None),
        ),
        out_specs=(P(("dp", "expert"), None), P(("dp", "expert"), None), P(("dp", "expert"))),
        check_vma=False,
    )
```
